128 devices in a mesh: tok: 8 (over x, core), head: 16 (over z, y).
Axes of the slice: x: 4, y: 4, z: 4, core: 2. Of those that a mesh axis runs over, the one named last changes fastest.
Arguments:
- hidden_in: bfloat16 [8192, 2048], P(('tok', 'head')), may hold values from -270 to 270, as said below
- cache_keys: bfloat16 [16384, 2048], P(('tok', 'head')), may hold values from -480 to 480, as said below
- cache_values: bfloat16 [16384, 2048], P(('tok', 'head')), may hold values from -6 to 6
- w_query: bfloat16 [2048, 2048], P(None, 'head'), may hold values from -0.3125 to 0.3125
- w_key: bfloat16 [2048, 2048], P(None, 'head'), may hold values from -0.125 to 0.125
- w_value: bfloat16 [2048, 2048], P(None, 'head'), may hold values from -0.125 to 0.125
- w_out: bfloat16 [2048, 2048], P('head'), may hold values from -0.375 to 0.375
- span_slot: int32 [16], replicated, may hold values from 0 to 15, each once
- span_start: int32 [16], replicated, may hold values from 0 to 16384, as said below
- recomp_rows: int32 [8192], replicated, may hold values from -1 to 16383, as said below
Outputs:
- update: bfloat16 [8192, 2048], P(('tok', 'head'))
- merged_keys: bfloat16 [16384, 2048], P('tok', 'head')
- merged_values: bfloat16 [16384, 2048], P('tok', 'head')
The draws below stay inside these ranges and needn't reach their ends.
Inputs may be any that keep to these rules, and one draw needn't show every extreme that they name: `hidden_in`: a custom float draw. `cache_keys`: a custom float draw. `span_slot`: each slot number appears once. `span_start`: ascending; slot s begins at least 1024 and at most 1088 positions after slot s - 1, slot 0 at most 64. `recomp_rows`: slot s belongs to block s // 64, which holds stored positions block * 128 to block * 128 + 127; a live slot names one of its own block's positions; within a block live slots come first, distinct and ascending; the number of live slots differs from block to block, and some block has all 64 slots live.
All inputs are finite; a program needn't handle non-finite values.
Results may differ from the reference program's by a relative error of at most 0.04.
The reference program's roundings to bfloat16 on the way (of `normed`, `queries`, `fresh_keys`, `fresh_values`, `shifted` and `attended`) count: a program that leaves them out, or rounds other values in their place, can miss the bound.
Values may be sent and summed in bfloat16 or wider, within the bound.
No kernel may reach another device: no remote copies, remote signals or barrier semaphores. Data moves between devices by JAX's collectives and lax.ppermute only.
A program may use at most 128 MiB of HBM per device.

```python
import math
import jax
import jax.numpy as jnp
from jax import lax

D = 2048
HEADS = 16
HDIM = 128
CH = 16
CL = 1024
GAP = 64
RMAX = 64
L = 16384
POS_DEV = 128
SLOTS = 8192


def draw_hidden_in(key, part):
    key_base, key_rows, key_columns, key_shift = jax.random.split(key, 4)
    base_draw = jnp.clip(jax.random.normal(key_base, (SLOTS, D), jnp.float32), -6.0, 6.0)
    row_scale = jnp.exp(jax.random.uniform(key_rows, (SLOTS, 1), jnp.float32, 0.0, math.log(10.0)))
    column_scale = jnp.exp(jax.random.uniform(key_columns, (1, D), jnp.float32, 0.0, math.log(4.0)))
    row_shift = jnp.clip(jax.random.normal(key_shift, (SLOTS, 1), jnp.float32), -3.0, 3.0)
    return (row_scale * (base_draw * column_scale + row_shift)).astype(jnp.bfloat16)


def draw_cache_keys(key, part):
    key_base = jax.random.fold_in(key, 0)
    base_draw = jnp.clip(jax.random.normal(key_base, (L, D), jnp.float32), -6.0, 6.0)
    return base_draw.astype(jnp.bfloat16)


def draw_span_start(key, part):
    gap_sizes = jax.random.randint(key, (CH,), 0, GAP + 1)
    return (jnp.arange(CH, dtype=jnp.int32) * CL + jnp.cumsum(gap_sizes)).astype(jnp.int32)


def draw_recomp_rows(key, part):
    blocks = SLOTS // RMAX
    key_counts, key_full, key_sparse, key_order = jax.random.split(key, 4)
    counts = jax.random.randint(key_counts, (blocks,), RMAX // 4, RMAX + 1)
    full_block = jax.random.randint(key_full, (), 0, blocks)
    sparse_block = (full_block + 1 + jax.random.randint(key_sparse, (), 0, blocks - 1)) % blocks
    counts = counts.at[sparse_block].set(RMAX // 4).at[full_block].set(RMAX)
    block_keys = jax.random.split(key_order, blocks)

    def fill_block(block_key, count_live, block_number):
        shuffled = jax.random.permutation(block_key, POS_DEV)[:RMAX]
        chosen = jnp.arange(RMAX, dtype=jnp.int32) < count_live
        ordered = jnp.sort(jnp.where(chosen, shuffled, POS_DEV))
        return jnp.where(ordered < POS_DEV, ordered + block_number * POS_DEV, -1).astype(jnp.int32)
    filled = jax.vmap(fill_block)(block_keys, counts, jnp.arange(blocks, dtype=jnp.int32))
    return filled.reshape(SLOTS).astype(jnp.int32)


def block_scale(own_key, shape, shards, low, high):
    gain, own = 1.0, jax.random.fold_in(own_key, 6)
    for dim, blocks in shards:
        steps = jnp.exp(jax.random.uniform(jax.random.fold_in(own, dim), (blocks,), jnp.float32, low / len(shards), high / len(shards)))
        gain = gain * jnp.repeat(steps, shape[dim] // blocks).reshape([-1 if axis == dim else 1 for axis in range(len(shape))])
    return gain


def gaussian(key, extent, deviation, reach, pieces=(), kind=jnp.bfloat16):
    factor_of = block_scale(key, extent, pieces, -0.22, 0.18) if pieces else 1.0
    array = jax.random.normal(key, extent, jnp.float32) * deviation * factor_of
    return jnp.minimum(jnp.maximum(array, -reach), reach).astype(kind)


def setup_inputs(seed: int = 0) -> dict:
    streams_of = jax.random.split(jax.random.key(seed), 11)
    return {
        "hidden_in": draw_hidden_in(jax.random.fold_in(streams_of[10], 71), 0),
        "cache_keys": draw_cache_keys(jax.random.fold_in(streams_of[10], 71), 0),
        "cache_values": gaussian(streams_of[2], (L, D), 1.0, 6.0, ((0, 128),)),
        "w_query": gaussian(streams_of[3], (D, D), (D // 6) ** -0.5, 0.3125, ((1, 16),)),
        "w_key": gaussian(streams_of[4], (D, D), D ** -0.5, 0.125, ((1, 16),)),
        "w_value": gaussian(streams_of[5], (D, D), D ** -0.5, 0.125, ((1, 16),)),
        "w_out": gaussian(streams_of[6], (D, D), (D // 8) ** -0.5, 0.375, ((0, 16),)),
        "span_slot": jax.random.permutation(streams_of[7], CH).astype(jnp.int32),
        "span_start": draw_span_start(jax.random.fold_in(streams_of[10], 71), 0),
        "recomp_rows": draw_recomp_rows(jax.random.fold_in(streams_of[10], 71), 0),
    }


theta = 10000.0
epsilon = 1e-05
negative = -1e+30
far_position = 1073741824

def rotate(values, angle_at):
    half_dim = values.shape[-1] // 2
    frequency = theta ** (-(jnp.arange(half_dim, dtype=jnp.float32) * (2.0 / values.shape[-1])))
    angles = angle_at.astype(jnp.float32)[:, None] * frequency[None, :]
    cosine = jnp.cos(angles)[:, None, :]
    sine_term = jnp.sin(angles)[:, None, :]
    first_half = values[..., :half_dim]
    second_half = values[..., half_dim:]
    return jnp.concatenate([first_half * cosine - second_half * sine_term, second_half * cosine + first_half * sine_term], axis=-1)

def layer_norm(hidden):
    values = hidden.astype(jnp.float32)
    center = values - lax.optimization_barrier(jnp.mean(values, axis=-1, keepdims=True))
    spread = lax.optimization_barrier(jnp.mean(center * center, axis=-1, keepdims=True))
    return (center * lax.rsqrt(spread + epsilon)).astype(jnp.bfloat16)

def new_positions(library, span_slot, span_start):
    span_index = jnp.clip(library // CL, 0, CH - 1)
    return span_start[span_slot[span_index]] + library % CL

def reference(hidden_in, cache_keys, cache_values, w_query, w_key, w_value, w_out, span_slot, span_start, recomp_rows):
    slot_count = recomp_rows.shape[0]
    is_live = recomp_rows >= 0
    normed = layer_norm(hidden_in)
    query_pos = new_positions(jnp.maximum(recomp_rows, 0), span_slot, span_start)
    queries = rotate(jnp.dot(normed, w_query, preferred_element_type=jnp.float32).reshape(slot_count, HEADS, HDIM), query_pos).astype(jnp.bfloat16)
    fresh_keys = rotate(jnp.dot(normed, w_key, preferred_element_type=jnp.float32).reshape(slot_count, HEADS, HDIM), query_pos).astype(jnp.bfloat16)
    fresh_values = jnp.dot(normed, w_value, preferred_element_type=jnp.float32).astype(jnp.bfloat16).reshape(slot_count, HEADS, HDIM)
    library = jnp.arange(L, dtype=jnp.int32)
    key_pos = new_positions(library, span_slot, span_start)
    shifted = rotate(cache_keys.astype(jnp.float32).reshape(L, HEADS, HDIM), key_pos - library % CL).astype(jnp.bfloat16)
    target = jnp.where(is_live, recomp_rows, L)
    merged_keys = shifted.at[target].set(fresh_keys, mode='drop')
    merged_values = cache_values.reshape(L, HEADS, HDIM).at[target].set(fresh_values, mode='drop')
    query_limit = jnp.where(is_live, query_pos, far_position)
    block_rows = math.gcd(slot_count, 512)
    score_scale = HDIM ** (-0.5)

    def one_head(operands):
        head_queries, head_keys, head_values = operands

        def one_block(block_operands):
            block_queries, block_limit = block_operands
            scores = jnp.dot(block_queries, head_keys.T, preferred_element_type=jnp.float32) * score_scale
            visible = key_pos[None, :] <= block_limit[:, None]
            scores = jnp.where(visible, scores, negative)
            row_peak = lax.optimization_barrier(jnp.max(scores, axis=-1, keepdims=True))
            weights = jnp.where(visible, jnp.exp(scores - row_peak), 0.0)
            row_total = lax.optimization_barrier(jnp.sum(weights, axis=-1, keepdims=True))
            summed = jnp.dot(weights.astype(jnp.bfloat16), head_values, preferred_element_type=jnp.float32)
            return (summed / row_total).astype(jnp.bfloat16)
        blocks_in = (head_queries.reshape(slot_count // block_rows, block_rows, HDIM), query_limit.reshape(slot_count // block_rows, block_rows))
        return lax.map(one_block, blocks_in).reshape(slot_count, HDIM)
    attended = lax.map(one_head, (queries.transpose(1, 0, 2), merged_keys.transpose(1, 0, 2), merged_values.transpose(1, 0, 2)))
    attended = attended.transpose(1, 0, 2).reshape(slot_count, HEADS * HDIM)
    update = jnp.dot(attended, w_out, preferred_element_type=jnp.float32)
    update = jnp.where(is_live[:, None], update, 0.0).astype(jnp.bfloat16)
    return (update, merged_keys.reshape(L, HEADS * HDIM), merged_values.reshape(L, HEADS * HDIM))
```

```python
import jax
import jax.numpy as jnp
from jax import lax
from jax.sharding import PartitionSpec as P

HDIM = 128
CH = 16
CL = 1024


theta = 10000.0
epsilon = 1e-05
negative = -1e30
far_position = 1073741824
key_block = 1024


def rotate(values, angle_at):
    half_dim = values.shape[-1] // 2
    frequency = theta ** (-(jnp.arange(half_dim, dtype=jnp.float32) * (2.0 / values.shape[-1])))
    angles = angle_at.astype(jnp.float32)[:, None] * frequency[None, :]
    cosine = jnp.cos(angles)[:, None, :]
    sine_term = jnp.sin(angles)[:, None, :]
    first_half = values[..., :half_dim]
    second_half = values[..., half_dim:]
    return jnp.concatenate(
        [
            first_half * cosine - second_half * sine_term,
            second_half * cosine + first_half * sine_term,
        ],
        axis=-1,
    )


def layer_norm(hidden):
    values = hidden.astype(jnp.float32)
    center = values - jnp.mean(values, axis=-1, keepdims=True)
    spread = jnp.mean(center * center, axis=-1, keepdims=True)
    return (center * lax.rsqrt(spread + epsilon)).astype(jnp.bfloat16)


def new_positions(library, span_slot, span_start):
    span_index = library // CL
    span_ids = jnp.arange(CH, dtype=jnp.int32)
    slot_index = jnp.sum(
        jnp.where(span_index[:, None] == span_ids[None, :], span_slot[None, :], 0), axis=1
    )
    start_pos = jnp.sum(
        jnp.where(slot_index[:, None] == span_ids[None, :], span_start[None, :], 0), axis=1
    )
    return start_pos + library % CL


def online_update(running, queries, query_limit, part_keys, part_values, part_pos):
    run_peak, run_total, run_sum = running
    scores = jnp.einsum(
        "qhd,khd->hqk", queries, part_keys, preferred_element_type=jnp.float32
    ) * HDIM ** (-0.5)
    visible = part_pos[None, None, :] <= query_limit[None, :, None]
    scores = jnp.where(visible, scores, negative)
    new_peak = jnp.maximum(run_peak, jnp.max(scores, axis=-1))
    factor = jnp.exp(run_peak - new_peak)
    weights = jnp.where(visible, jnp.exp(scores - new_peak[..., None]), 0.0)
    run_total = run_total * factor + jnp.sum(weights, axis=-1)
    added = jnp.einsum(
        "hqk,khd->hqd",
        weights.astype(jnp.bfloat16),
        part_values,
        preferred_element_type=jnp.float32,
    )
    run_sum = run_sum * factor[..., None] + added
    return (new_peak, run_total, run_sum)


def local(
    hidden_in,
    cache_keys,
    cache_values,
    w_query,
    w_key,
    w_value,
    w_out,
    span_slot,
    span_start,
    recomp_rows,
):
    head_count = lax.axis_size("head")
    tok_count = lax.axis_size("tok")
    tok_index = lax.axis_index("tok")
    head_index = lax.axis_index("head")
    own_rows = hidden_in.shape[0]
    head_width = w_query.shape[1]
    local_heads = head_width // HDIM
    group_rows = own_rows * head_count
    normed = layer_norm(hidden_in)
    w_joined = jnp.concatenate([w_query, w_key, w_value], axis=1)
    projected = jnp.dot(
        lax.all_gather(normed, "head", axis=0, tiled=True),
        w_joined,
        preferred_element_type=jnp.float32,
    )
    group_slots = lax.dynamic_slice_in_dim(recomp_rows, tok_index * group_rows, group_rows)
    is_live = group_slots >= 0
    query_pos = new_positions(jnp.maximum(group_slots, 0), span_slot, span_start)
    queries = rotate(
        projected[:, :head_width].reshape(group_rows, local_heads, HDIM), query_pos
    ).astype(jnp.bfloat16)
    fresh_keys = rotate(
        projected[:, head_width : 2 * head_width].reshape(group_rows, local_heads, HDIM), query_pos
    ).astype(jnp.bfloat16)
    fresh_values = (
        projected[:, 2 * head_width :].astype(jnp.bfloat16).reshape(group_rows, local_heads, HDIM)
    )
    moved_keys, moved_values = (
        lax.all_to_all(cache_keys, "head", split_axis=1, concat_axis=0, tiled=True),
        lax.all_to_all(cache_values, "head", split_axis=1, concat_axis=0, tiled=True),
    )
    block_len = moved_keys.shape[0]
    library = tok_index * block_len + jnp.arange(block_len, dtype=jnp.int32)
    key_pos = new_positions(library, span_slot, span_start)
    shifted = rotate(
        moved_keys.astype(jnp.float32).reshape(block_len, local_heads, HDIM), key_pos - library % CL
    ).astype(jnp.bfloat16)
    target = jnp.where(is_live, group_slots - tok_index * block_len, block_len)
    merged_keys = shifted.at[target].set(fresh_keys, mode="drop").reshape(block_len, head_width)
    merged_values = (
        moved_values.reshape(block_len, local_heads, HDIM)
        .at[target]
        .set(fresh_values, mode="drop")
        .reshape(block_len, head_width)
    )
    query_limit = jnp.where(is_live, query_pos, far_position)
    state = (
        jnp.full((local_heads, group_rows), negative, jnp.float32),
        jnp.zeros((local_heads, group_rows), jnp.float32),
        jnp.zeros((local_heads, group_rows, HDIM), jnp.float32),
    )
    half = block_len // 2
    forward_pairs = [(i, (i + 1) % tok_count) for i in range(tok_count)]
    backward_pairs = [(i, (i - 1) % tok_count) for i in range(tok_count)]
    offsets = jnp.arange(half, dtype=jnp.int32)

    def absorb(turn, ahead, behind, state):
        ahead_start = ((tok_index - turn) % tok_count) * block_len
        behind_start = ((tok_index + turn) % tok_count) * block_len + half
        for (part_keys, part_values), start in ((ahead, ahead_start), (behind, behind_start)):
            part_pos = new_positions(start + offsets, span_slot, span_start)
            state = online_update(
                state,
                queries,
                query_limit,
                part_keys.reshape(half, local_heads, HDIM),
                part_values.reshape(half, local_heads, HDIM),
                part_pos,
            )
        return state

    ahead = (merged_keys[:half], merged_values[:half])
    behind = (merged_keys[half:], merged_values[half:])
    for turn in range(tok_count):
        if turn + 1 < tok_count:
            next_ahead = lax.ppermute(ahead, "tok", forward_pairs)
            next_behind = lax.ppermute(behind, "tok", backward_pairs)
        state = absorb(turn, ahead, behind, state)
        if turn + 1 < tok_count:
            ahead, behind = next_ahead, next_behind
    row_peak, row_total, summed = state
    attended = (
        (summed / row_total[..., None])
        .astype(jnp.bfloat16)
        .transpose(1, 0, 2)
        .reshape(group_rows, head_width)
    )
    out_width = w_out.shape[1]
    column_half = tok_index % 2
    w_late, _ = lax.optimization_barrier((w_out, projected))
    own_half = lax.all_gather(
        lax.dynamic_slice_in_dim(w_late, column_half * (out_width // 2), out_width // 2, 1),
        "head",
        axis=0,
        tiled=True,
    )
    partner_pairs = [(i, i ^ 1) for i in range(tok_count)]
    other_half = lax.ppermute(own_half, "tok", partner_pairs)
    slot_rows = lax.all_to_all(attended, "head", split_axis=0, concat_axis=1, tiled=True)
    first = jnp.where(column_half == 0, own_half, other_half)
    second = jnp.where(column_half == 0, other_half, own_half)
    update = jnp.concatenate(
        [
            jnp.dot(slot_rows, first, preferred_element_type=jnp.float32),
            jnp.dot(slot_rows, second, preferred_element_type=jnp.float32),
        ],
        axis=1,
    )
    own_slots = lax.dynamic_slice_in_dim(
        recomp_rows, (tok_index * head_count + head_index) * own_rows, own_rows
    )
    update = jnp.where((own_slots >= 0)[:, None], update, 0.0).astype(jnp.bfloat16)
    return (update, merged_keys, merged_values)


def solution(mesh):
    in_specs = (
        P(("tok", "head"), None),
        P(("tok", "head"), None),
        P(("tok", "head"), None),
        P(None, "head"),
        P(None, "head"),
        P(None, "head"),
        P("head", None),
        P(),
        P(),
        P(),
    )
    out_specs = (P(("tok", "head"), None), P("tok", "head"), P("tok", "head"))
    return jax.shard_map(local, mesh=mesh, in_specs=in_specs, out_specs=out_specs, check_vma=False)
```

```python
import jax
import jax.numpy as jnp
from jax import lax
from jax.sharding import PartitionSpec as P

HDIM = 128
CH = 16
CL = 1024


theta = 10000.0
epsilon = 1e-05
negative = -1e30
far_position = 1073741824
key_block = 1024


def rotate(values, angle_at):
    half_dim = values.shape[-1] // 2
    frequency = theta ** (-(jnp.arange(half_dim, dtype=jnp.float32) * (2.0 / values.shape[-1])))
    angles = angle_at.astype(jnp.float32)[:, None] * frequency[None, :]
    cosine = jnp.cos(angles)[:, None, :]
    sine_term = jnp.sin(angles)[:, None, :]
    first_half = values[..., :half_dim]
    second_half = values[..., half_dim:]
    return jnp.concatenate(
        [
            first_half * cosine - second_half * sine_term,
            second_half * cosine + first_half * sine_term,
        ],
        axis=-1,
    )


def layer_norm(hidden):
    values = hidden.astype(jnp.float32)
    center = values - jnp.mean(values, axis=-1, keepdims=True)
    spread = jnp.mean(center * center, axis=-1, keepdims=True)
    return (center * lax.rsqrt(spread + epsilon)).astype(jnp.bfloat16)


def new_positions(library, span_slot, span_start):
    span_index = library // CL
    span_ids = jnp.arange(CH, dtype=jnp.int32)
    slot_index = jnp.sum(
        jnp.where(span_index[:, None] == span_ids[None, :], span_slot[None, :], 0), axis=1
    )
    start_pos = jnp.sum(
        jnp.where(slot_index[:, None] == span_ids[None, :], span_start[None, :], 0), axis=1
    )
    return start_pos + library % CL


def online_update(running, queries, query_limit, part_keys, part_values, part_pos):
    run_peak, run_total, run_sum = running
    scores = jnp.einsum(
        "qhd,khd->hqk", queries, part_keys, preferred_element_type=jnp.float32
    ) * HDIM ** (-0.5)
    visible = part_pos[None, None, :] <= query_limit[None, :, None]
    scores = jnp.where(visible, scores, negative)
    new_peak = jnp.maximum(run_peak, jnp.max(scores, axis=-1))
    factor = jnp.exp(run_peak - new_peak)
    weights = jnp.where(visible, jnp.exp(scores - new_peak[..., None]), 0.0)
    run_total = run_total * factor + jnp.sum(weights, axis=-1)
    added = jnp.einsum(
        "hqk,khd->hqd",
        weights.astype(jnp.bfloat16),
        part_values,
        preferred_element_type=jnp.float32,
    )
    run_sum = run_sum * factor[..., None] + added
    return (new_peak, run_total, run_sum)


def local(
    hidden_in,
    cache_keys,
    cache_values,
    w_query,
    w_key,
    w_value,
    w_out,
    span_slot,
    span_start,
    recomp_rows,
):
    head_count = lax.axis_size("head")
    tok_count = lax.axis_size("tok")
    tok_index = lax.axis_index("tok")
    head_index = lax.axis_index("head")
    own_rows = hidden_in.shape[0]
    head_width = w_query.shape[1]
    local_heads = head_width // HDIM
    group_rows = own_rows * head_count
    normed = layer_norm(hidden_in)
    w_joined = jnp.concatenate([w_query, w_key, w_value], axis=1)
    projected = jnp.dot(
        lax.all_gather(normed, "head", axis=0, tiled=True),
        w_joined,
        preferred_element_type=jnp.float32,
    )
    group_slots = lax.dynamic_slice_in_dim(recomp_rows, tok_index * group_rows, group_rows)
    is_live = group_slots >= 0
    query_pos = new_positions(jnp.maximum(group_slots, 0), span_slot, span_start)
    queries = rotate(
        projected[:, :head_width].reshape(group_rows, local_heads, HDIM), query_pos
    ).astype(jnp.bfloat16)
    fresh_keys = rotate(
        projected[:, head_width : 2 * head_width].reshape(group_rows, local_heads, HDIM), query_pos
    ).astype(jnp.bfloat16)
    fresh_values = (
        projected[:, 2 * head_width :].astype(jnp.bfloat16).reshape(group_rows, local_heads, HDIM)
    )
    moved_keys, moved_values = (
        lax.all_to_all(cache_keys, "head", split_axis=1, concat_axis=0, tiled=True),
        lax.all_to_all(cache_values, "head", split_axis=1, concat_axis=0, tiled=True),
    )
    block_len = moved_keys.shape[0]
    library = tok_index * block_len + jnp.arange(block_len, dtype=jnp.int32)
    key_pos = new_positions(library, span_slot, span_start)
    shifted = rotate(
        moved_keys.astype(jnp.float32).reshape(block_len, local_heads, HDIM), key_pos - library % CL
    ).astype(jnp.bfloat16)
    target = jnp.where(is_live, group_slots - tok_index * block_len, block_len)
    merged_keys = shifted.at[target].set(fresh_keys, mode="drop").reshape(block_len, head_width)
    merged_values = (
        moved_values.reshape(block_len, local_heads, HDIM)
        .at[target]
        .set(fresh_values, mode="drop")
        .reshape(block_len, head_width)
    )
    query_limit = jnp.where(is_live, query_pos, far_position)
    state = (
        jnp.full((local_heads, group_rows), negative, jnp.float32),
        jnp.zeros((local_heads, group_rows), jnp.float32),
        jnp.zeros((local_heads, group_rows, HDIM), jnp.float32),
    )
    half = block_len // 2
    forward_pairs = [(i, (i + 1) % tok_count) for i in range(tok_count)]
    backward_pairs = [(i, (i - 1) % tok_count) for i in range(tok_count)]
    offsets = jnp.arange(half, dtype=jnp.int32)

    def absorb(turn, ahead, behind, state):
        ahead_start = ((tok_index - turn) % tok_count) * block_len
        behind_start = ((tok_index + turn) % tok_count) * block_len + half
        for part, start in ((ahead, ahead_start), (behind, behind_start)):
            part_keys, part_values = part[:, :head_width], part[:, head_width:]
            part_pos = new_positions(start + offsets, span_slot, span_start)
            state = online_update(
                state,
                queries,
                query_limit,
                part_keys.reshape(half, local_heads, HDIM),
                part_values.reshape(half, local_heads, HDIM),
                part_pos,
            )
        return state

    merged_both = jnp.concatenate([merged_keys, merged_values], axis=1)
    ahead, behind = merged_both[:half], merged_both[half:]
    for turn in range(tok_count):
        if turn + 1 < tok_count:
            next_ahead = lax.ppermute(ahead, "tok", forward_pairs)
            next_behind = lax.ppermute(behind, "tok", backward_pairs)
        state = absorb(turn, ahead, behind, state)
        if turn + 1 < tok_count:
            ahead, behind = next_ahead, next_behind
    row_peak, row_total, summed = state
    attended = (
        (summed / row_total[..., None])
        .astype(jnp.bfloat16)
        .transpose(1, 0, 2)
        .reshape(group_rows, head_width)
    )
    out_width = w_out.shape[1]
    column_half = tok_index % 2
    w_late, _ = lax.optimization_barrier((w_out, projected))
    own_half = lax.all_gather(
        lax.dynamic_slice_in_dim(w_late, column_half * (out_width // 2), out_width // 2, 1),
        "head",
        axis=0,
        tiled=True,
    )
    partner_pairs = [(i, i ^ 1) for i in range(tok_count)]
    other_half = lax.ppermute(own_half, "tok", partner_pairs)
    slot_rows = lax.all_to_all(attended, "head", split_axis=0, concat_axis=1, tiled=True)
    first = jnp.where(column_half == 0, own_half, other_half)
    second = jnp.where(column_half == 0, other_half, own_half)
    update = jnp.concatenate(
        [
            jnp.dot(slot_rows, first, preferred_element_type=jnp.float32),
            jnp.dot(slot_rows, second, preferred_element_type=jnp.float32),
        ],
        axis=1,
    )
    own_slots = lax.dynamic_slice_in_dim(
        recomp_rows, (tok_index * head_count + head_index) * own_rows, own_rows
    )
    update = jnp.where((own_slots >= 0)[:, None], update, 0.0).astype(jnp.bfloat16)
    return (update, merged_keys, merged_values)


def solution(mesh):
    in_specs = (
        P(("tok", "head"), None),
        P(("tok", "head"), None),
        P(("tok", "head"), None),
        P(None, "head"),
        P(None, "head"),
        P(None, "head"),
        P("head", None),
        P(),
        P(),
        P(),
    )
    out_specs = (P(("tok", "head"), None), P("tok", "head"), P("tok", "head"))
    return jax.shard_map(local, mesh=mesh, in_specs=in_specs, out_specs=out_specs, check_vma=False)
```

```python
import jax
import jax.numpy as jnp
from jax import lax
from jax.sharding import PartitionSpec as P
from jax.experimental import pallas as pl
from jax.experimental.pallas import tpu as pltpu

HDIM = 128
CH = 16
CL = 1024


theta = 10000.0
epsilon = 1e-05
negative = -1e30
far_position = 1073741824
key_block = 1024


def rotate(values, angle_at):
    half_dim = values.shape[-1] // 2
    frequency = theta ** (-(jnp.arange(half_dim, dtype=jnp.float32) * (2.0 / values.shape[-1])))
    angles = angle_at.astype(jnp.float32)[:, None] * frequency[None, :]
    cosine = jnp.cos(angles)[:, None, :]
    sine_term = jnp.sin(angles)[:, None, :]
    first_half = values[..., :half_dim]
    second_half = values[..., half_dim:]
    return jnp.concatenate(
        [
            first_half * cosine - second_half * sine_term,
            second_half * cosine + first_half * sine_term,
        ],
        axis=-1,
    )


def layer_norm(hidden):
    values = hidden.astype(jnp.float32)
    center = values - jnp.mean(values, axis=-1, keepdims=True)
    spread = jnp.mean(center * center, axis=-1, keepdims=True)
    return (center * lax.rsqrt(spread + epsilon)).astype(jnp.bfloat16)


def new_positions(library, span_slot, span_start):
    span_index = library // CL
    span_ids = jnp.arange(CH, dtype=jnp.int32)
    slot_index = jnp.sum(
        jnp.where(span_index[:, None] == span_ids[None, :], span_slot[None, :], 0), axis=1
    )
    start_pos = jnp.sum(
        jnp.where(slot_index[:, None] == span_ids[None, :], span_start[None, :], 0), axis=1
    )
    return start_pos + library % CL


query_tile = 512
key_tile = 2048


def attention_kernel(q_ref, limit_ref, kv_ref, pos_ref, out_ref, peak_ref, total_ref, sum_ref):
    key_step = pl.program_id(1)

    @pl.when(key_step == 0)
    def _():
        peak_ref[...] = jnp.full(peak_ref.shape, negative, jnp.float32)
        total_ref[...] = jnp.zeros(total_ref.shape, jnp.float32)
        sum_ref[...] = jnp.zeros(sum_ref.shape, jnp.float32)

    width = q_ref.shape[1]
    part_keys = kv_ref[:, :width]
    part_values = kv_ref[:, width:]
    scores = lax.dot_general(
        q_ref[...], part_keys, (((1,), (1,)), ((), ())), preferred_element_type=jnp.float32
    ) * (width ** -0.5)
    visible = pos_ref[...] <= limit_ref[...]
    scores = jnp.where(visible, scores, negative)
    old_peak = peak_ref[...]
    new_peak = jnp.maximum(old_peak, jnp.max(scores, axis=1, keepdims=True))
    factor = jnp.exp(old_peak - new_peak)
    weights = jnp.where(visible, jnp.exp(scores - new_peak), 0.0)
    total_ref[...] = total_ref[...] * factor + jnp.sum(weights, axis=1, keepdims=True)
    sum_ref[...] = sum_ref[...] * factor + jnp.dot(
        weights.astype(jnp.bfloat16), part_values, preferred_element_type=jnp.float32
    )
    peak_ref[...] = new_peak

    @pl.when(key_step == pl.num_programs(1) - 1)
    def _():
        out_ref[...] = (sum_ref[...] / total_ref[...]).astype(out_ref.dtype)


def attend(queries, query_limit, keys_values, key_pos):
    rows, width = queries.shape
    count = keys_values.shape[0]
    q_tile = min(query_tile, rows)
    k_tile = min(key_tile, count)
    return pl.pallas_call(
        attention_kernel,
        grid=(rows // q_tile, count // k_tile),
        in_specs=[
            pl.BlockSpec((q_tile, width), lambda i, j: (i, 0)),
            pl.BlockSpec((q_tile, 1), lambda i, j: (i, 0)),
            pl.BlockSpec((k_tile, 2 * width), lambda i, j: (j, 0)),
            pl.BlockSpec((1, k_tile), lambda i, j: (0, j)),
        ],
        out_specs=pl.BlockSpec((q_tile, width), lambda i, j: (i, 0)),
        out_shape=jax.ShapeDtypeStruct((rows, width), jnp.bfloat16),
        scratch_shapes=[
            pltpu.VMEM((q_tile, 1), jnp.float32),
            pltpu.VMEM((q_tile, 1), jnp.float32),
            pltpu.VMEM((q_tile, width), jnp.float32),
        ],
        compiler_params=pltpu.CompilerParams(
            dimension_semantics=("arbitrary", "arbitrary"), vmem_limit_bytes=48 * 1024 * 1024
        ),
    )(queries, query_limit.reshape(rows, 1), keys_values, key_pos.reshape(1, count))


def online_update(running, queries, query_limit, part_keys, part_values, part_pos):
    run_peak, run_total, run_sum = running
    scores = jnp.einsum(
        "qhd,khd->hqk", queries, part_keys, preferred_element_type=jnp.float32
    ) * HDIM ** (-0.5)
    visible = part_pos[None, None, :] <= query_limit[None, :, None]
    scores = jnp.where(visible, scores, negative)
    new_peak = jnp.maximum(run_peak, jnp.max(scores, axis=-1))
    factor = jnp.exp(run_peak - new_peak)
    weights = jnp.where(visible, jnp.exp(scores - new_peak[..., None]), 0.0)
    run_total = run_total * factor + jnp.sum(weights, axis=-1)
    added = jnp.einsum(
        "hqk,khd->hqd",
        weights.astype(jnp.bfloat16),
        part_values,
        preferred_element_type=jnp.float32,
    )
    run_sum = run_sum * factor[..., None] + added
    return (new_peak, run_total, run_sum)


def local(
    hidden_in,
    cache_keys,
    cache_values,
    w_query,
    w_key,
    w_value,
    w_out,
    span_slot,
    span_start,
    recomp_rows,
):
    head_count = lax.axis_size("head")
    tok_count = lax.axis_size("tok")
    tok_index = lax.axis_index("tok")
    head_index = lax.axis_index("head")
    own_rows = hidden_in.shape[0]
    head_width = w_query.shape[1]
    local_heads = head_width // HDIM
    group_rows = own_rows * head_count
    normed = layer_norm(hidden_in)
    w_joined = jnp.concatenate([w_query, w_key, w_value], axis=1)
    projected = jnp.dot(
        lax.all_gather(normed, "head", axis=0, tiled=True),
        w_joined,
        preferred_element_type=jnp.float32,
    )
    group_slots = lax.dynamic_slice_in_dim(recomp_rows, tok_index * group_rows, group_rows)
    is_live = group_slots >= 0
    query_pos = new_positions(jnp.maximum(group_slots, 0), span_slot, span_start)
    queries = rotate(
        projected[:, :head_width].reshape(group_rows, local_heads, HDIM), query_pos
    ).astype(jnp.bfloat16)
    fresh_keys = rotate(
        projected[:, head_width : 2 * head_width].reshape(group_rows, local_heads, HDIM), query_pos
    ).astype(jnp.bfloat16)
    fresh_values = (
        projected[:, 2 * head_width :].astype(jnp.bfloat16).reshape(group_rows, local_heads, HDIM)
    )
    moved_keys, moved_values = (
        lax.all_to_all(cache_keys, "head", split_axis=1, concat_axis=0, tiled=True),
        lax.all_to_all(cache_values, "head", split_axis=1, concat_axis=0, tiled=True),
    )
    block_len = moved_keys.shape[0]
    library = tok_index * block_len + jnp.arange(block_len, dtype=jnp.int32)
    key_pos = new_positions(library, span_slot, span_start)
    shifted = rotate(
        moved_keys.astype(jnp.float32).reshape(block_len, local_heads, HDIM), key_pos - library % CL
    ).astype(jnp.bfloat16)
    target = jnp.where(is_live, group_slots - tok_index * block_len, block_len)
    merged_keys = shifted.at[target].set(fresh_keys, mode="drop").reshape(block_len, head_width)
    merged_values = (
        moved_values.reshape(block_len, local_heads, HDIM)
        .at[target]
        .set(fresh_values, mode="drop")
        .reshape(block_len, head_width)
    )
    query_limit = jnp.where(is_live, query_pos, far_position)
    merged_both = jnp.concatenate([merged_keys, merged_values], axis=1)
    all_both = lax.all_gather(merged_both, "tok", axis=0, tiled=True)
    count_keys = all_both.shape[0]
    all_pos = new_positions(jnp.arange(count_keys, dtype=jnp.int32), span_slot, span_start)
    attended = jnp.concatenate(
        [
            attend(
                queries[:, head],
                query_limit,
                jnp.concatenate(
                    [
                        all_both[:, head * HDIM : (head + 1) * HDIM],
                        all_both[:, head_width + head * HDIM : head_width + (head + 1) * HDIM],
                    ],
                    axis=1,
                ) if local_heads > 1 else all_both,
                all_pos,
            )
            for head in range(local_heads)
        ],
        axis=1,
    )
    out_width = w_out.shape[1]
    column_half = tok_index % 2
    w_late, _ = lax.optimization_barrier((w_out, projected))
    own_half = lax.all_to_all(
        jnp.tile(
            lax.dynamic_slice_in_dim(w_late, column_half * (out_width // 2), out_width // 2, 1),
            (head_count, 1),
        ),
        "head",
        split_axis=0,
        concat_axis=0,
        tiled=True,
    )
    partner_pairs = [(i, i ^ 1) for i in range(tok_count)]
    other_half = lax.ppermute(own_half, "tok", partner_pairs)
    slot_rows = lax.all_to_all(attended, "head", split_axis=0, concat_axis=1, tiled=True)
    first = jnp.where(column_half == 0, own_half, other_half)
    second = jnp.where(column_half == 0, other_half, own_half)
    update = jnp.concatenate(
        [
            jnp.dot(slot_rows, first, preferred_element_type=jnp.float32),
            jnp.dot(slot_rows, second, preferred_element_type=jnp.float32),
        ],
        axis=1,
    )
    own_slots = lax.dynamic_slice_in_dim(
        recomp_rows, (tok_index * head_count + head_index) * own_rows, own_rows
    )
    update = jnp.where((own_slots >= 0)[:, None], update, 0.0).astype(jnp.bfloat16)
    return (update, merged_keys, merged_values)


def solution(mesh):
    in_specs = (
        P(("tok", "head"), None),
        P(("tok", "head"), None),
        P(("tok", "head"), None),
        P(None, "head"),
        P(None, "head"),
        P(None, "head"),
        P("head", None),
        P(),
        P(),
        P(),
    )
    out_specs = (P(("tok", "head"), None), P("tok", "head"), P("tok", "head"))
    return jax.shard_map(local, mesh=mesh, in_specs=in_specs, out_specs=out_specs, check_vma=False)
```

```python
import functools

import jax
import jax.numpy as jnp
from jax import lax
from jax.sharding import PartitionSpec as P
from jax.experimental import pallas as pl
from jax.experimental.pallas import tpu as pltpu

HDIM = 128
CH = 16
CL = 1024


theta = 10000.0
epsilon = 1e-05
negative = -1e30
far_position = 1073741824
key_block = 1024


def rotate(values, angle_at):
    half_dim = values.shape[-1] // 2
    frequency = theta ** (-(jnp.arange(half_dim, dtype=jnp.float32) * (2.0 / values.shape[-1])))
    angles = angle_at.astype(jnp.float32)[:, None] * frequency[None, :]
    cosine = jnp.cos(angles)[:, None, :]
    sine_term = jnp.sin(angles)[:, None, :]
    first_half = values[..., :half_dim]
    second_half = values[..., half_dim:]
    return jnp.concatenate(
        [
            first_half * cosine - second_half * sine_term,
            second_half * cosine + first_half * sine_term,
        ],
        axis=-1,
    )


def layer_norm(hidden):
    values = hidden.astype(jnp.float32)
    center = values - jnp.mean(values, axis=-1, keepdims=True)
    spread = jnp.mean(center * center, axis=-1, keepdims=True)
    return (center * lax.rsqrt(spread + epsilon)).astype(jnp.bfloat16)


def new_positions(library, span_slot, span_start):
    span_index = library // CL
    span_ids = jnp.arange(CH, dtype=jnp.int32)
    slot_index = jnp.sum(
        jnp.where(span_index[:, None] == span_ids[None, :], span_slot[None, :], 0), axis=1
    )
    start_pos = jnp.sum(
        jnp.where(slot_index[:, None] == span_ids[None, :], span_start[None, :], 0), axis=1
    )
    return start_pos + library % CL


query_tile = 512
key_tile = 2048


def attention_kernel(*refs, carried, final):
    if carried:
        q_ref, limit_ref, kv_ref, pos_ref, peak_in, total_in, sum_in = refs[:7]
        rest = refs[7:]
    else:
        q_ref, limit_ref, kv_ref, pos_ref = refs[:4]
        rest = refs[4:]
    outs = rest[:1] if final else rest[:3]
    peak_ref, total_ref, sum_ref = rest[len(outs) :]
    key_step = pl.program_id(1)

    @pl.when(key_step == 0)
    def _():
        if carried:
            peak_ref[...] = peak_in[...]
            total_ref[...] = total_in[...]
            sum_ref[...] = sum_in[...]
        else:
            peak_ref[...] = jnp.full(peak_ref.shape, negative, jnp.float32)
            total_ref[...] = jnp.zeros(total_ref.shape, jnp.float32)
            sum_ref[...] = jnp.zeros(sum_ref.shape, jnp.float32)

    width = q_ref.shape[1]
    part_keys = kv_ref[:, :width]
    part_values = kv_ref[:, width:]
    scores = lax.dot_general(
        q_ref[...], part_keys, (((1,), (1,)), ((), ())), preferred_element_type=jnp.float32
    ) * (width ** -0.5)
    visible = pos_ref[...] <= limit_ref[...]
    scores = jnp.where(visible, scores, negative)
    old_peak = peak_ref[...]
    new_peak = jnp.maximum(old_peak, jnp.max(scores, axis=1, keepdims=True))
    factor = jnp.exp(old_peak - new_peak)
    weights = jnp.where(visible, jnp.exp(scores - new_peak), 0.0)
    total_ref[...] = total_ref[...] * factor + jnp.sum(weights, axis=1, keepdims=True)
    sum_ref[...] = sum_ref[...] * factor + jnp.dot(
        weights.astype(jnp.bfloat16), part_values, preferred_element_type=jnp.float32
    )
    peak_ref[...] = new_peak

    @pl.when(key_step == pl.num_programs(1) - 1)
    def _():
        if final:
            outs[0][...] = (sum_ref[...] / total_ref[...]).astype(outs[0].dtype)
        else:
            outs[0][...] = peak_ref[...]
            outs[1][...] = total_ref[...]
            outs[2][...] = sum_ref[...]


def attend(queries, query_limit, keys_values, key_pos, carry=None, final=True):
    rows, width = queries.shape
    count = keys_values.shape[0]
    q_tile = min(query_tile, rows)
    k_tile = min(key_tile, count)
    row_spec = pl.BlockSpec((q_tile, 1), lambda i, j: (i, 0))
    wide_spec = pl.BlockSpec((q_tile, width), lambda i, j: (i, 0))
    in_specs = [
        wide_spec,
        row_spec,
        pl.BlockSpec((k_tile, 2 * width), lambda i, j: (j, 0)),
        pl.BlockSpec((1, k_tile), lambda i, j: (0, j)),
    ]
    operands = [queries, query_limit.reshape(rows, 1), keys_values, key_pos.reshape(1, count)]
    if carry is not None:
        in_specs += [row_spec, row_spec, wide_spec]
        operands += list(carry)
    if final:
        out_specs = wide_spec
        out_shape = jax.ShapeDtypeStruct((rows, width), jnp.bfloat16)
    else:
        out_specs = (row_spec, row_spec, wide_spec)
        out_shape = (
            jax.ShapeDtypeStruct((rows, 1), jnp.float32),
            jax.ShapeDtypeStruct((rows, 1), jnp.float32),
            jax.ShapeDtypeStruct((rows, width), jnp.float32),
        )
    return pl.pallas_call(
        functools.partial(attention_kernel, carried=carry is not None, final=final),
        grid=(rows // q_tile, count // k_tile),
        in_specs=in_specs,
        out_specs=out_specs,
        out_shape=out_shape,
        scratch_shapes=[
            pltpu.VMEM((q_tile, 1), jnp.float32),
            pltpu.VMEM((q_tile, 1), jnp.float32),
            pltpu.VMEM((q_tile, width), jnp.float32),
        ],
        compiler_params=pltpu.CompilerParams(
            dimension_semantics=("arbitrary", "arbitrary"), vmem_limit_bytes=48 * 1024 * 1024
        ),
    )(*operands)


def online_update(running, queries, query_limit, part_keys, part_values, part_pos):
    run_peak, run_total, run_sum = running
    scores = jnp.einsum(
        "qhd,khd->hqk", queries, part_keys, preferred_element_type=jnp.float32
    ) * HDIM ** (-0.5)
    visible = part_pos[None, None, :] <= query_limit[None, :, None]
    scores = jnp.where(visible, scores, negative)
    new_peak = jnp.maximum(run_peak, jnp.max(scores, axis=-1))
    factor = jnp.exp(run_peak - new_peak)
    weights = jnp.where(visible, jnp.exp(scores - new_peak[..., None]), 0.0)
    run_total = run_total * factor + jnp.sum(weights, axis=-1)
    added = jnp.einsum(
        "hqk,khd->hqd",
        weights.astype(jnp.bfloat16),
        part_values,
        preferred_element_type=jnp.float32,
    )
    run_sum = run_sum * factor[..., None] + added
    return (new_peak, run_total, run_sum)


def local(
    hidden_in,
    cache_keys,
    cache_values,
    w_query,
    w_key,
    w_value,
    w_out,
    span_slot,
    span_start,
    recomp_rows,
):
    head_count = lax.axis_size("head")
    tok_count = lax.axis_size("tok")
    tok_index = lax.axis_index("tok")
    head_index = lax.axis_index("head")
    own_rows = hidden_in.shape[0]
    head_width = w_query.shape[1]
    local_heads = head_width // HDIM
    group_rows = own_rows * head_count
    normed = layer_norm(hidden_in)
    w_joined = jnp.concatenate([w_query, w_key, w_value], axis=1)
    projected = jnp.dot(
        lax.all_gather(normed, "head", axis=0, tiled=True),
        w_joined,
        preferred_element_type=jnp.float32,
    )
    group_slots = lax.dynamic_slice_in_dim(recomp_rows, tok_index * group_rows, group_rows)
    is_live = group_slots >= 0
    query_pos = new_positions(jnp.maximum(group_slots, 0), span_slot, span_start)
    queries = rotate(
        projected[:, :head_width].reshape(group_rows, local_heads, HDIM), query_pos
    ).astype(jnp.bfloat16)
    fresh_keys = rotate(
        projected[:, head_width : 2 * head_width].reshape(group_rows, local_heads, HDIM), query_pos
    ).astype(jnp.bfloat16)
    fresh_values = (
        projected[:, 2 * head_width :].astype(jnp.bfloat16).reshape(group_rows, local_heads, HDIM)
    )
    moved_keys, moved_values = (
        lax.all_to_all(cache_keys, "head", split_axis=1, concat_axis=0, tiled=True),
        lax.all_to_all(cache_values, "head", split_axis=1, concat_axis=0, tiled=True),
    )
    block_len = moved_keys.shape[0]
    library = tok_index * block_len + jnp.arange(block_len, dtype=jnp.int32)
    key_pos = new_positions(library, span_slot, span_start)
    shifted = rotate(
        moved_keys.astype(jnp.float32).reshape(block_len, local_heads, HDIM), key_pos - library % CL
    ).astype(jnp.bfloat16)
    target = jnp.where(is_live, group_slots - tok_index * block_len, block_len)
    merged_keys = shifted.at[target].set(fresh_keys, mode="drop").reshape(block_len, head_width)
    merged_values = (
        moved_values.reshape(block_len, local_heads, HDIM)
        .at[target]
        .set(fresh_values, mode="drop")
        .reshape(block_len, head_width)
    )
    query_limit = jnp.where(is_live, query_pos, far_position)
    merged_both = jnp.concatenate([merged_keys, merged_values], axis=1)
    half = block_len // 2
    first_both = lax.all_gather(merged_both[:half], "tok", axis=0, tiled=True)
    second_both = lax.all_gather(merged_both[half:], "tok", axis=0, tiled=True)
    sources = jnp.arange(tok_count, dtype=jnp.int32)[:, None] * block_len
    offsets = jnp.arange(half, dtype=jnp.int32)[None, :]
    first_pos = new_positions((sources + offsets).reshape(-1), span_slot, span_start)
    second_pos = new_positions((sources + half + offsets).reshape(-1), span_slot, span_start)

    def head_columns(both, head):
        if local_heads == 1:
            return both
        return jnp.concatenate(
            [
                both[:, head * HDIM : (head + 1) * HDIM],
                both[:, head_width + head * HDIM : head_width + (head + 1) * HDIM],
            ],
            axis=1,
        )

    attended_heads = []
    for head in range(local_heads):
        carry = attend(
            queries[:, head], query_limit, head_columns(first_both, head), first_pos, final=False
        )
        attended_heads.append(
            attend(queries[:, head], query_limit, head_columns(second_both, head), second_pos, carry)
        )
    attended = jnp.concatenate(attended_heads, axis=1)
    out_width = w_out.shape[1]
    column_half = tok_index % 2
    after_gather = -(jnp.abs(second_both[0, 0]) * 0)
    own_half = lax.all_gather(
        lax.dynamic_slice_in_dim(w_out, column_half * (out_width // 2), out_width // 2, 1)
        + after_gather,
        "head",
        axis=0,
        tiled=True,
    )
    partner_pairs = [(i, i ^ 1) for i in range(tok_count)]
    slot_rows = lax.all_to_all(attended, "head", split_axis=0, concat_axis=1, tiled=True)
    partner_rows = lax.ppermute(slot_rows, "tok", partner_pairs)
    both_parts = jnp.dot(
        jnp.concatenate([slot_rows, partner_rows], axis=0), own_half, preferred_element_type=jnp.float32
    ).astype(jnp.bfloat16)
    mine = both_parts[:own_rows]
    other = lax.ppermute(both_parts[own_rows:], "tok", partner_pairs)
    update = jnp.where(
        column_half == 0,
        jnp.concatenate([mine, other], axis=1),
        jnp.concatenate([other, mine], axis=1),
    )
    own_slots = lax.dynamic_slice_in_dim(
        recomp_rows, (tok_index * head_count + head_index) * own_rows, own_rows
    )
    update = jnp.where((own_slots >= 0)[:, None], update, 0.0).astype(jnp.bfloat16)
    return (update, merged_keys, merged_values)


def solution(mesh):
    in_specs = (
        P(("tok", "head"), None),
        P(("tok", "head"), None),
        P(("tok", "head"), None),
        P(None, "head"),
        P(None, "head"),
        P(None, "head"),
        P("head", None),
        P(),
        P(),
        P(),
    )
    out_specs = (P(("tok", "head"), None), P("tok", "head"), P("tok", "head"))
    return jax.shard_map(local, mesh=mesh, in_specs=in_specs, out_specs=out_specs, check_vma=False)
```

```python
import functools

import jax
import jax.numpy as jnp
from jax import lax
from jax.sharding import PartitionSpec as P
from jax.experimental import pallas as pl
from jax.experimental.pallas import tpu as pltpu

HDIM = 128
CH = 16
CL = 1024


theta = 10000.0
epsilon = 1e-05
negative = -1e30
far_position = 1073741824
key_block = 1024


def rotate(values, angle_at):
    half_dim = values.shape[-1] // 2
    frequency = theta ** (-(jnp.arange(half_dim, dtype=jnp.float32) * (2.0 / values.shape[-1])))
    angles = angle_at.astype(jnp.float32)[:, None] * frequency[None, :]
    cosine = jnp.cos(angles)[:, None, :]
    sine_term = jnp.sin(angles)[:, None, :]
    first_half = values[..., :half_dim]
    second_half = values[..., half_dim:]
    return jnp.concatenate(
        [
            first_half * cosine - second_half * sine_term,
            second_half * cosine + first_half * sine_term,
        ],
        axis=-1,
    )


def layer_norm(hidden):
    values = hidden.astype(jnp.float32)
    center = values - jnp.mean(values, axis=-1, keepdims=True)
    spread = jnp.mean(center * center, axis=-1, keepdims=True)
    return (center * lax.rsqrt(spread + epsilon)).astype(jnp.bfloat16)


def new_positions(library, span_slot, span_start):
    span_index = library // CL
    span_ids = jnp.arange(CH, dtype=jnp.int32)
    slot_index = jnp.sum(
        jnp.where(span_index[:, None] == span_ids[None, :], span_slot[None, :], 0), axis=1
    )
    start_pos = jnp.sum(
        jnp.where(slot_index[:, None] == span_ids[None, :], span_start[None, :], 0), axis=1
    )
    return start_pos + library % CL


query_tile = 512
key_tile = 2048


def attention_kernel(*refs, carried, final):
    if carried:
        q_ref, limit_ref, kv_ref, pos_ref, peak_in, total_in, sum_in = refs[:7]
        rest = refs[7:]
    else:
        q_ref, limit_ref, kv_ref, pos_ref = refs[:4]
        rest = refs[4:]
    outs = rest[:1] if final else rest[:3]
    peak_ref, total_ref, sum_ref = rest[len(outs) :]
    key_step = pl.program_id(1)

    @pl.when(key_step == 0)
    def _():
        if carried:
            peak_ref[...] = peak_in[...]
            total_ref[...] = total_in[...]
            sum_ref[...] = sum_in[...]
        else:
            peak_ref[...] = jnp.full(peak_ref.shape, negative, jnp.float32)
            total_ref[...] = jnp.zeros(total_ref.shape, jnp.float32)
            sum_ref[...] = jnp.zeros(sum_ref.shape, jnp.float32)

    width = q_ref.shape[1]
    part_keys = kv_ref[:, :width]
    part_values = kv_ref[:, width:]
    scores = lax.dot_general(
        q_ref[...], part_keys, (((1,), (1,)), ((), ())), preferred_element_type=jnp.float32
    ) * (width ** -0.5)
    visible = pos_ref[...] <= limit_ref[...]
    scores = jnp.where(visible, scores, negative)
    old_peak = peak_ref[...]
    new_peak = jnp.maximum(old_peak, jnp.max(scores, axis=1, keepdims=True))
    factor = jnp.exp(old_peak - new_peak)
    weights = jnp.where(visible, jnp.exp(scores - new_peak), 0.0)
    total_ref[...] = total_ref[...] * factor + jnp.sum(weights, axis=1, keepdims=True)
    sum_ref[...] = sum_ref[...] * factor + jnp.dot(
        weights.astype(jnp.bfloat16), part_values, preferred_element_type=jnp.float32
    )
    peak_ref[...] = new_peak

    @pl.when(key_step == pl.num_programs(1) - 1)
    def _():
        if final:
            outs[0][...] = (sum_ref[...] / total_ref[...]).astype(outs[0].dtype)
        else:
            outs[0][...] = peak_ref[...]
            outs[1][...] = total_ref[...]
            outs[2][...] = sum_ref[...]


def attend(queries, query_limit, keys_values, key_pos, carry=None, final=True):
    rows, width = queries.shape
    count = keys_values.shape[0]
    q_tile = min(query_tile, rows)
    k_tile = min(key_tile, count)
    row_spec = pl.BlockSpec((q_tile, 1), lambda i, j: (i, 0))
    wide_spec = pl.BlockSpec((q_tile, width), lambda i, j: (i, 0))
    in_specs = [
        wide_spec,
        row_spec,
        pl.BlockSpec((k_tile, 2 * width), lambda i, j: (j, 0)),
        pl.BlockSpec((1, k_tile), lambda i, j: (0, j)),
    ]
    operands = [queries, query_limit.reshape(rows, 1), keys_values, key_pos.reshape(1, count)]
    if carry is not None:
        in_specs += [row_spec, row_spec, wide_spec]
        operands += list(carry)
    if final:
        out_specs = wide_spec
        out_shape = jax.ShapeDtypeStruct((rows, width), jnp.bfloat16)
    else:
        out_specs = (row_spec, row_spec, wide_spec)
        out_shape = (
            jax.ShapeDtypeStruct((rows, 1), jnp.float32),
            jax.ShapeDtypeStruct((rows, 1), jnp.float32),
            jax.ShapeDtypeStruct((rows, width), jnp.float32),
        )
    return pl.pallas_call(
        functools.partial(attention_kernel, carried=carry is not None, final=final),
        grid=(rows // q_tile, count // k_tile),
        in_specs=in_specs,
        out_specs=out_specs,
        out_shape=out_shape,
        scratch_shapes=[
            pltpu.VMEM((q_tile, 1), jnp.float32),
            pltpu.VMEM((q_tile, 1), jnp.float32),
            pltpu.VMEM((q_tile, width), jnp.float32),
        ],
        compiler_params=pltpu.CompilerParams(
            dimension_semantics=("arbitrary", "arbitrary"), vmem_limit_bytes=48 * 1024 * 1024
        ),
    )(*operands)


def online_update(running, queries, query_limit, part_keys, part_values, part_pos):
    run_peak, run_total, run_sum = running
    scores = jnp.einsum(
        "qhd,khd->hqk", queries, part_keys, preferred_element_type=jnp.float32
    ) * HDIM ** (-0.5)
    visible = part_pos[None, None, :] <= query_limit[None, :, None]
    scores = jnp.where(visible, scores, negative)
    new_peak = jnp.maximum(run_peak, jnp.max(scores, axis=-1))
    factor = jnp.exp(run_peak - new_peak)
    weights = jnp.where(visible, jnp.exp(scores - new_peak[..., None]), 0.0)
    run_total = run_total * factor + jnp.sum(weights, axis=-1)
    added = jnp.einsum(
        "hqk,khd->hqd",
        weights.astype(jnp.bfloat16),
        part_values,
        preferred_element_type=jnp.float32,
    )
    run_sum = run_sum * factor[..., None] + added
    return (new_peak, run_total, run_sum)


def local(
    hidden_in,
    cache_keys,
    cache_values,
    w_query,
    w_key,
    w_value,
    w_out,
    span_slot,
    span_start,
    recomp_rows,
):
    head_count = lax.axis_size("head")
    tok_count = lax.axis_size("tok")
    tok_index = lax.axis_index("tok")
    head_index = lax.axis_index("head")
    own_rows = hidden_in.shape[0]
    head_width = w_query.shape[1]
    local_heads = head_width // HDIM
    group_rows = own_rows * head_count
    normed = layer_norm(hidden_in)
    w_joined = jnp.concatenate([w_query, w_key, w_value], axis=1)
    projected = jnp.dot(
        lax.all_gather(normed, "head", axis=0, tiled=True),
        w_joined,
        preferred_element_type=jnp.float32,
    )
    group_slots = lax.dynamic_slice_in_dim(recomp_rows, tok_index * group_rows, group_rows)
    is_live = group_slots >= 0
    query_pos = new_positions(jnp.maximum(group_slots, 0), span_slot, span_start)
    queries = rotate(
        projected[:, :head_width].reshape(group_rows, local_heads, HDIM), query_pos
    ).astype(jnp.bfloat16)
    fresh_keys = rotate(
        projected[:, head_width : 2 * head_width].reshape(group_rows, local_heads, HDIM), query_pos
    ).astype(jnp.bfloat16)
    fresh_values = (
        projected[:, 2 * head_width :].astype(jnp.bfloat16).reshape(group_rows, local_heads, HDIM)
    )
    moved_keys, moved_values = (
        lax.all_to_all(cache_keys, "head", split_axis=1, concat_axis=0, tiled=True),
        lax.all_to_all(cache_values, "head", split_axis=1, concat_axis=0, tiled=True),
    )
    block_len = moved_keys.shape[0]
    library = tok_index * block_len + jnp.arange(block_len, dtype=jnp.int32)
    key_pos = new_positions(library, span_slot, span_start)
    shifted = rotate(
        moved_keys.astype(jnp.float32).reshape(block_len, local_heads, HDIM), key_pos - library % CL
    ).astype(jnp.bfloat16)
    target = jnp.where(is_live, group_slots - tok_index * block_len, block_len)
    merged_keys = shifted.at[target].set(fresh_keys, mode="drop").reshape(block_len, head_width)
    merged_values = (
        moved_values.reshape(block_len, local_heads, HDIM)
        .at[target]
        .set(fresh_values, mode="drop")
        .reshape(block_len, head_width)
    )
    query_limit = jnp.where(is_live, query_pos, far_position)
    merged_both = jnp.concatenate([merged_keys, merged_values], axis=1)
    all_both = lax.all_gather(merged_both, "tok", axis=0, tiled=True)
    count_keys = all_both.shape[0]
    all_pos = new_positions(jnp.arange(count_keys, dtype=jnp.int32), span_slot, span_start)

    def head_columns(both, head):
        if local_heads == 1:
            return both
        return jnp.concatenate(
            [
                both[:, head * HDIM : (head + 1) * HDIM],
                both[:, head_width + head * HDIM : head_width + (head + 1) * HDIM],
            ],
            axis=1,
        )

    attended_heads = [
        attend(queries[:, head], query_limit, head_columns(all_both, head), all_pos)
        for head in range(local_heads)
    ]
    attended = jnp.concatenate(attended_heads, axis=1)
    out_width = w_out.shape[1]
    column_half = tok_index % 2
    after_gather = -(jnp.abs(all_both[0, 0]) * 0)
    own_half = lax.all_gather(
        lax.dynamic_slice_in_dim(w_out, column_half * (out_width // 2), out_width // 2, 1)
        + after_gather,
        "head",
        axis=0,
        tiled=True,
    )
    partner_pairs = [(i, i ^ 1) for i in range(tok_count)]
    slot_rows = lax.all_to_all(attended, "head", split_axis=0, concat_axis=1, tiled=True)
    partner_rows = lax.ppermute(slot_rows, "tok", partner_pairs)
    both_parts = jnp.dot(
        jnp.concatenate([slot_rows, partner_rows], axis=0), own_half, preferred_element_type=jnp.float32
    ).astype(jnp.bfloat16)
    mine = both_parts[:own_rows]
    other = lax.ppermute(both_parts[own_rows:], "tok", partner_pairs)
    update = jnp.where(
        column_half == 0,
        jnp.concatenate([mine, other], axis=1),
        jnp.concatenate([other, mine], axis=1),
    )
    own_slots = lax.dynamic_slice_in_dim(
        recomp_rows, (tok_index * head_count + head_index) * own_rows, own_rows
    )
    update = jnp.where((own_slots >= 0)[:, None], update, 0.0).astype(jnp.bfloat16)
    return (update, merged_keys, merged_values)


def solution(mesh):
    in_specs = (
        P(("tok", "head"), None),
        P(("tok", "head"), None),
        P(("tok", "head"), None),
        P(None, "head"),
        P(None, "head"),
        P(None, "head"),
        P("head", None),
        P(),
        P(),
        P(),
    )
    out_specs = (P(("tok", "head"), None), P("tok", "head"), P("tok", "head"))
    return jax.shard_map(local, mesh=mesh, in_specs=in_specs, out_specs=out_specs, check_vma=False)
```

```python
import functools

import jax
import jax.numpy as jnp
from jax import lax
from jax.sharding import PartitionSpec as P
from jax.experimental import pallas as pl
from jax.experimental.pallas import tpu as pltpu

HDIM = 128
CH = 16
CL = 1024


theta = 10000.0
epsilon = 1e-05
negative = -1e30
far_position = 1073741824
key_block = 1024


def rotate(values, angle_at):
    half_dim = values.shape[-1] // 2
    frequency = theta ** (-(jnp.arange(half_dim, dtype=jnp.float32) * (2.0 / values.shape[-1])))
    angles = angle_at.astype(jnp.float32)[:, None] * frequency[None, :]
    cosine = jnp.cos(angles)[:, None, :]
    sine_term = jnp.sin(angles)[:, None, :]
    first_half = values[..., :half_dim]
    second_half = values[..., half_dim:]
    return jnp.concatenate(
        [
            first_half * cosine - second_half * sine_term,
            second_half * cosine + first_half * sine_term,
        ],
        axis=-1,
    )


def layer_norm(hidden):
    values = hidden.astype(jnp.float32)
    center = values - jnp.mean(values, axis=-1, keepdims=True)
    spread = jnp.mean(center * center, axis=-1, keepdims=True)
    return (center * lax.rsqrt(spread + epsilon)).astype(jnp.bfloat16)


def new_positions(library, span_slot, span_start):
    span_index = library // CL
    span_ids = jnp.arange(CH, dtype=jnp.int32)
    slot_index = jnp.sum(
        jnp.where(span_index[:, None] == span_ids[None, :], span_slot[None, :], 0), axis=1
    )
    start_pos = jnp.sum(
        jnp.where(slot_index[:, None] == span_ids[None, :], span_start[None, :], 0), axis=1
    )
    return start_pos + library % CL


query_tile = 512
key_tile = 2048


def attention_kernel(
    low_limit, high_limit, low_pos, high_pos, q_ref, limit_ref, kv_ref, pos_ref, out_ref,
    peak_ref, total_ref, sum_ref,
):
    query_step = pl.program_id(0)
    key_step = pl.program_id(1)

    @pl.when(key_step == 0)
    def _():
        peak_ref[...] = jnp.full(peak_ref.shape, negative, jnp.float32)
        total_ref[...] = jnp.zeros(total_ref.shape, jnp.float32)
        sum_ref[...] = jnp.zeros(sum_ref.shape, jnp.float32)

    def absorb(masked):
        width = q_ref.shape[1]
        part_keys = kv_ref[:, :width]
        part_values = kv_ref[:, width:]
        scores = lax.dot_general(
            q_ref[...], part_keys, (((1,), (1,)), ((), ())), preferred_element_type=jnp.float32
        ) * (width ** -0.5)
        if masked:
            visible = pos_ref[...] <= limit_ref[...]
            scores = jnp.where(visible, scores, negative)
        old_peak = peak_ref[...]
        new_peak = jnp.maximum(old_peak, jnp.max(scores, axis=1, keepdims=True))
        factor = jnp.exp(old_peak - new_peak)
        weights = jnp.exp(scores - new_peak)
        if masked:
            weights = jnp.where(visible, weights, 0.0)
        total_ref[...] = total_ref[...] * factor + jnp.sum(weights, axis=1, keepdims=True)
        sum_ref[...] = sum_ref[...] * factor + jnp.dot(
            weights.astype(jnp.bfloat16), part_values, preferred_element_type=jnp.float32
        )
        peak_ref[...] = new_peak

    all_seen = high_pos[key_step] <= low_limit[query_step]
    none_seen = low_pos[key_step] > high_limit[query_step]

    @pl.when(all_seen)
    def _():
        absorb(False)

    @pl.when(jnp.logical_and(jnp.logical_not(all_seen), jnp.logical_not(none_seen)))
    def _():
        absorb(True)

    @pl.when(key_step == pl.num_programs(1) - 1)
    def _():
        out_ref[...] = (sum_ref[...] / total_ref[...]).astype(out_ref.dtype)


def attend(queries, query_limit, keys_values, key_pos):
    rows, width = queries.shape
    count = keys_values.shape[0]
    q_tile = min(query_tile, rows)
    k_tile = min(key_tile, count)
    tiled_limit = query_limit.reshape(rows // q_tile, q_tile)
    tiled_pos = key_pos.reshape(count // k_tile, k_tile)
    grid_spec = pltpu.PrefetchScalarGridSpec(
        num_scalar_prefetch=4,
        grid=(rows // q_tile, count // k_tile),
        in_specs=[
            pl.BlockSpec((q_tile, width), lambda i, j, *_: (i, 0)),
            pl.BlockSpec((q_tile, 1), lambda i, j, *_: (i, 0)),
            pl.BlockSpec((k_tile, 2 * width), lambda i, j, *_: (j, 0)),
            pl.BlockSpec((1, k_tile), lambda i, j, *_: (0, j)),
        ],
        out_specs=pl.BlockSpec((q_tile, width), lambda i, j, *_: (i, 0)),
        scratch_shapes=[
            pltpu.VMEM((q_tile, 1), jnp.float32),
            pltpu.VMEM((q_tile, 1), jnp.float32),
            pltpu.VMEM((q_tile, width), jnp.float32),
        ],
    )
    return pl.pallas_call(
        attention_kernel,
        grid_spec=grid_spec,
        out_shape=jax.ShapeDtypeStruct((rows, width), jnp.bfloat16),
        compiler_params=pltpu.CompilerParams(
            dimension_semantics=("arbitrary", "arbitrary"), vmem_limit_bytes=48 * 1024 * 1024
        ),
    )(
        jnp.min(tiled_limit, axis=1),
        jnp.max(tiled_limit, axis=1),
        jnp.min(tiled_pos, axis=1),
        jnp.max(tiled_pos, axis=1),
        queries,
        query_limit.reshape(rows, 1),
        keys_values,
        key_pos.reshape(1, count),
    )


def online_update(running, queries, query_limit, part_keys, part_values, part_pos):
    run_peak, run_total, run_sum = running
    scores = jnp.einsum(
        "qhd,khd->hqk", queries, part_keys, preferred_element_type=jnp.float32
    ) * HDIM ** (-0.5)
    visible = part_pos[None, None, :] <= query_limit[None, :, None]
    scores = jnp.where(visible, scores, negative)
    new_peak = jnp.maximum(run_peak, jnp.max(scores, axis=-1))
    factor = jnp.exp(run_peak - new_peak)
    weights = jnp.where(visible, jnp.exp(scores - new_peak[..., None]), 0.0)
    run_total = run_total * factor + jnp.sum(weights, axis=-1)
    added = jnp.einsum(
        "hqk,khd->hqd",
        weights.astype(jnp.bfloat16),
        part_values,
        preferred_element_type=jnp.float32,
    )
    run_sum = run_sum * factor[..., None] + added
    return (new_peak, run_total, run_sum)


def local(
    hidden_in,
    cache_keys,
    cache_values,
    w_query,
    w_key,
    w_value,
    w_out,
    span_slot,
    span_start,
    recomp_rows,
):
    head_count = lax.axis_size("head")
    tok_count = lax.axis_size("tok")
    tok_index = lax.axis_index("tok")
    head_index = lax.axis_index("head")
    own_rows = hidden_in.shape[0]
    head_width = w_query.shape[1]
    local_heads = head_width // HDIM
    group_rows = own_rows * head_count
    normed = layer_norm(hidden_in)
    w_joined = jnp.concatenate([w_query, w_key, w_value], axis=1)
    projected = jnp.dot(
        lax.all_gather(normed, "head", axis=0, tiled=True),
        w_joined,
        preferred_element_type=jnp.float32,
    )
    group_slots = lax.dynamic_slice_in_dim(recomp_rows, tok_index * group_rows, group_rows)
    is_live = group_slots >= 0
    query_pos = new_positions(jnp.maximum(group_slots, 0), span_slot, span_start)
    queries = rotate(
        projected[:, :head_width].reshape(group_rows, local_heads, HDIM), query_pos
    ).astype(jnp.bfloat16)
    fresh_keys = rotate(
        projected[:, head_width : 2 * head_width].reshape(group_rows, local_heads, HDIM), query_pos
    ).astype(jnp.bfloat16)
    fresh_values = (
        projected[:, 2 * head_width :].astype(jnp.bfloat16).reshape(group_rows, local_heads, HDIM)
    )
    moved_keys, moved_values = (
        lax.all_to_all(cache_keys, "head", split_axis=1, concat_axis=0, tiled=True),
        lax.all_to_all(cache_values, "head", split_axis=1, concat_axis=0, tiled=True),
    )
    block_len = moved_keys.shape[0]
    library = tok_index * block_len + jnp.arange(block_len, dtype=jnp.int32)
    key_pos = new_positions(library, span_slot, span_start)
    shifted = rotate(
        moved_keys.astype(jnp.float32).reshape(block_len, local_heads, HDIM), key_pos - library % CL
    ).astype(jnp.bfloat16)
    target = jnp.where(is_live, group_slots - tok_index * block_len, block_len)
    merged_keys = shifted.at[target].set(fresh_keys, mode="drop").reshape(block_len, head_width)
    merged_values = (
        moved_values.reshape(block_len, local_heads, HDIM)
        .at[target]
        .set(fresh_values, mode="drop")
        .reshape(block_len, head_width)
    )
    query_limit = jnp.where(is_live, query_pos, far_position)
    merged_both = jnp.concatenate([merged_keys, merged_values], axis=1)
    all_both = lax.all_gather(merged_both, "tok", axis=0, tiled=True)
    count_keys = all_both.shape[0]
    all_pos = new_positions(jnp.arange(count_keys, dtype=jnp.int32), span_slot, span_start)

    def head_columns(both, head):
        if local_heads == 1:
            return both
        return jnp.concatenate(
            [
                both[:, head * HDIM : (head + 1) * HDIM],
                both[:, head_width + head * HDIM : head_width + (head + 1) * HDIM],
            ],
            axis=1,
        )

    attended_heads = [
        attend(queries[:, head], query_limit, head_columns(all_both, head), all_pos)
        for head in range(local_heads)
    ]
    attended = jnp.concatenate(attended_heads, axis=1)
    out_width = w_out.shape[1]
    column_half = tok_index % 2
    after_gather = -(jnp.abs(all_both[0, 0]) * 0)
    own_half = lax.all_gather(
        lax.dynamic_slice_in_dim(w_out, column_half * (out_width // 2), out_width // 2, 1)
        + after_gather,
        "head",
        axis=0,
        tiled=True,
    )
    partner_pairs = [(i, i ^ 1) for i in range(tok_count)]
    slot_rows = lax.all_to_all(attended, "head", split_axis=0, concat_axis=1, tiled=True)
    partner_rows = lax.ppermute(slot_rows, "tok", partner_pairs)
    both_parts = jnp.dot(
        jnp.concatenate([slot_rows, partner_rows], axis=0), own_half, preferred_element_type=jnp.float32
    ).astype(jnp.bfloat16)
    mine = both_parts[:own_rows]
    other = lax.ppermute(both_parts[own_rows:], "tok", partner_pairs)
    update = jnp.where(
        column_half == 0,
        jnp.concatenate([mine, other], axis=1),
        jnp.concatenate([other, mine], axis=1),
    )
    own_slots = lax.dynamic_slice_in_dim(
        recomp_rows, (tok_index * head_count + head_index) * own_rows, own_rows
    )
    update = jnp.where((own_slots >= 0)[:, None], update, 0.0).astype(jnp.bfloat16)
    return (update, merged_keys, merged_values)


def solution(mesh):
    in_specs = (
        P(("tok", "head"), None),
        P(("tok", "head"), None),
        P(("tok", "head"), None),
        P(None, "head"),
        P(None, "head"),
        P(None, "head"),
        P("head", None),
        P(),
        P(),
        P(),
    )
    out_specs = (P(("tok", "head"), None), P("tok", "head"), P("tok", "head"))
    return jax.shard_map(local, mesh=mesh, in_specs=in_specs, out_specs=out_specs, check_vma=False)
```

```python
import functools

import jax
import jax.numpy as jnp
from jax import lax
from jax.sharding import PartitionSpec as P
from jax.experimental import pallas as pl
from jax.experimental.pallas import tpu as pltpu

HDIM = 128
CH = 16
CL = 1024


theta = 10000.0
epsilon = 1e-05
negative = -1e30
far_position = 1073741824
key_block = 1024


def rotate(values, angle_at):
    half_dim = values.shape[-1] // 2
    frequency = theta ** (-(jnp.arange(half_dim, dtype=jnp.float32) * (2.0 / values.shape[-1])))
    angles = angle_at.astype(jnp.float32)[:, None] * frequency[None, :]
    cosine = jnp.cos(angles)[:, None, :]
    sine_term = jnp.sin(angles)[:, None, :]
    first_half = values[..., :half_dim]
    second_half = values[..., half_dim:]
    return jnp.concatenate(
        [
            first_half * cosine - second_half * sine_term,
            second_half * cosine + first_half * sine_term,
        ],
        axis=-1,
    )


def layer_norm(hidden):
    values = hidden.astype(jnp.float32)
    center = values - jnp.mean(values, axis=-1, keepdims=True)
    spread = jnp.mean(center * center, axis=-1, keepdims=True)
    return (center * lax.rsqrt(spread + epsilon)).astype(jnp.bfloat16)


def new_positions(library, span_slot, span_start):
    span_index = library // CL
    span_ids = jnp.arange(CH, dtype=jnp.int32)
    slot_index = jnp.sum(
        jnp.where(span_index[:, None] == span_ids[None, :], span_slot[None, :], 0), axis=1
    )
    start_pos = jnp.sum(
        jnp.where(slot_index[:, None] == span_ids[None, :], span_start[None, :], 0), axis=1
    )
    return start_pos + library % CL


query_tile = 256
key_tile = 4096


def attention_kernel(
    live_count, low_limit, high_limit, low_pos, high_pos, q_ref, limit_ref, kv_ref, pos_ref, out_ref,
    peak_ref, total_ref, sum_ref,
):
    query_step = pl.program_id(0)
    key_step = pl.program_id(1)

    @pl.when(key_step == 0)
    def _():
        peak_ref[...] = jnp.full(peak_ref.shape, negative, jnp.float32)
        total_ref[...] = jnp.zeros(total_ref.shape, jnp.float32)
        sum_ref[...] = jnp.zeros(sum_ref.shape, jnp.float32)

    def absorb(masked):
        width = q_ref.shape[1]
        part_keys = kv_ref[:, :width]
        part_values = kv_ref[:, width:]
        scores = lax.dot_general(
            q_ref[...], part_keys, (((1,), (1,)), ((), ())), preferred_element_type=jnp.float32
        ) * (width ** -0.5)
        if masked:
            visible = pos_ref[...] <= limit_ref[...]
            scores = jnp.where(visible, scores, negative)
        old_peak = peak_ref[...]
        new_peak = jnp.maximum(old_peak, jnp.max(scores, axis=1, keepdims=True))
        factor = jnp.exp(old_peak - new_peak)
        weights = jnp.exp(scores - new_peak)
        if masked:
            weights = jnp.where(visible, weights, 0.0)
        total_ref[...] = total_ref[...] * factor + jnp.sum(weights, axis=1, keepdims=True)
        sum_ref[...] = sum_ref[...] * factor + jnp.dot(
            weights.astype(jnp.bfloat16), part_values, preferred_element_type=jnp.float32
        )
        peak_ref[...] = new_peak

    any_live = live_count[0] > query_step * q_ref.shape[0]
    all_seen = jnp.logical_and(any_live, high_pos[key_step] <= low_limit[query_step])
    none_seen = jnp.logical_or(
        jnp.logical_not(any_live), low_pos[key_step] > high_limit[query_step]
    )

    @pl.when(all_seen)
    def _():
        absorb(False)

    @pl.when(jnp.logical_and(jnp.logical_not(all_seen), jnp.logical_not(none_seen)))
    def _():
        absorb(True)

    @pl.when(key_step == pl.num_programs(1) - 1)
    def _():
        total = total_ref[...]
        out_ref[...] = jnp.where(total > 0, sum_ref[...] / total, 0.0).astype(out_ref.dtype)


def attend(queries, query_limit, keys_values, key_pos, live_count):
    rows, width = queries.shape
    count = keys_values.shape[0]
    q_tile = min(query_tile, rows)
    k_tile = min(key_tile, count)
    tiled_limit = query_limit.reshape(rows // q_tile, q_tile)
    tiled_pos = key_pos.reshape(count // k_tile, k_tile)
    grid_spec = pltpu.PrefetchScalarGridSpec(
        num_scalar_prefetch=5,
        grid=(rows // q_tile, count // k_tile),
        in_specs=[
            pl.BlockSpec((q_tile, width), lambda i, j, *_: (i, 0)),
            pl.BlockSpec((q_tile, 1), lambda i, j, *_: (i, 0)),
            pl.BlockSpec((k_tile, 2 * width), lambda i, j, *_: (j, 0)),
            pl.BlockSpec((1, k_tile), lambda i, j, *_: (0, j)),
        ],
        out_specs=pl.BlockSpec((q_tile, width), lambda i, j, *_: (i, 0)),
        scratch_shapes=[
            pltpu.VMEM((q_tile, 1), jnp.float32),
            pltpu.VMEM((q_tile, 1), jnp.float32),
            pltpu.VMEM((q_tile, width), jnp.float32),
        ],
    )
    return pl.pallas_call(
        attention_kernel,
        grid_spec=grid_spec,
        out_shape=jax.ShapeDtypeStruct((rows, width), jnp.bfloat16),
        compiler_params=pltpu.CompilerParams(
            dimension_semantics=("arbitrary", "arbitrary"), vmem_limit_bytes=48 * 1024 * 1024
        ),
    )(
        live_count.reshape(1),
        jnp.min(tiled_limit, axis=1),
        jnp.max(tiled_limit, axis=1),
        jnp.min(tiled_pos, axis=1),
        jnp.max(tiled_pos, axis=1),
        queries,
        query_limit.reshape(rows, 1),
        keys_values,
        key_pos.reshape(1, count),
    )


def online_update(running, queries, query_limit, part_keys, part_values, part_pos):
    run_peak, run_total, run_sum = running
    scores = jnp.einsum(
        "qhd,khd->hqk", queries, part_keys, preferred_element_type=jnp.float32
    ) * HDIM ** (-0.5)
    visible = part_pos[None, None, :] <= query_limit[None, :, None]
    scores = jnp.where(visible, scores, negative)
    new_peak = jnp.maximum(run_peak, jnp.max(scores, axis=-1))
    factor = jnp.exp(run_peak - new_peak)
    weights = jnp.where(visible, jnp.exp(scores - new_peak[..., None]), 0.0)
    run_total = run_total * factor + jnp.sum(weights, axis=-1)
    added = jnp.einsum(
        "hqk,khd->hqd",
        weights.astype(jnp.bfloat16),
        part_values,
        preferred_element_type=jnp.float32,
    )
    run_sum = run_sum * factor[..., None] + added
    return (new_peak, run_total, run_sum)


def local(
    hidden_in,
    cache_keys,
    cache_values,
    w_query,
    w_key,
    w_value,
    w_out,
    span_slot,
    span_start,
    recomp_rows,
):
    head_count = lax.axis_size("head")
    tok_count = lax.axis_size("tok")
    tok_index = lax.axis_index("tok")
    head_index = lax.axis_index("head")
    own_rows = hidden_in.shape[0]
    head_width = w_query.shape[1]
    local_heads = head_width // HDIM
    group_rows = own_rows * head_count
    normed = layer_norm(hidden_in)
    w_joined = jnp.concatenate([w_query, w_key, w_value], axis=1)
    projected = jnp.dot(
        lax.all_gather(normed, "head", axis=0, tiled=True),
        w_joined,
        preferred_element_type=jnp.float32,
    )
    group_slots = lax.dynamic_slice_in_dim(recomp_rows, tok_index * group_rows, group_rows)
    is_live = group_slots >= 0
    query_pos = new_positions(jnp.maximum(group_slots, 0), span_slot, span_start)
    queries = rotate(
        projected[:, :head_width].reshape(group_rows, local_heads, HDIM), query_pos
    ).astype(jnp.bfloat16)
    fresh_keys = rotate(
        projected[:, head_width : 2 * head_width].reshape(group_rows, local_heads, HDIM), query_pos
    ).astype(jnp.bfloat16)
    fresh_values = (
        projected[:, 2 * head_width :].astype(jnp.bfloat16).reshape(group_rows, local_heads, HDIM)
    )
    moved_keys, moved_values = (
        lax.all_to_all(cache_keys, "head", split_axis=1, concat_axis=0, tiled=True),
        lax.all_to_all(cache_values, "head", split_axis=1, concat_axis=0, tiled=True),
    )
    block_len = moved_keys.shape[0]
    library = tok_index * block_len + jnp.arange(block_len, dtype=jnp.int32)
    key_pos = new_positions(library, span_slot, span_start)
    shifted = rotate(
        moved_keys.astype(jnp.float32).reshape(block_len, local_heads, HDIM), key_pos - library % CL
    ).astype(jnp.bfloat16)
    target = jnp.where(is_live, group_slots - tok_index * block_len, block_len)
    merged_keys = shifted.at[target].set(fresh_keys, mode="drop").reshape(block_len, head_width)
    merged_values = (
        moved_values.reshape(block_len, local_heads, HDIM)
        .at[target]
        .set(fresh_values, mode="drop")
        .reshape(block_len, head_width)
    )
    query_limit = jnp.where(is_live, query_pos, far_position)
    merged_both = jnp.concatenate([merged_keys, merged_values], axis=1)
    all_both = lax.all_gather(merged_both, "tok", axis=0, tiled=True)
    count_keys = all_both.shape[0]
    all_pos = new_positions(jnp.arange(count_keys, dtype=jnp.int32), span_slot, span_start)

    def head_columns(both, head):
        if local_heads == 1:
            return both
        return jnp.concatenate(
            [
                both[:, head * HDIM : (head + 1) * HDIM],
                both[:, head_width + head * HDIM : head_width + (head + 1) * HDIM],
            ],
            axis=1,
        )

    order = jnp.argsort(jnp.where(is_live, 0, 1), stable=True)
    restore = jnp.argsort(order)
    live_count = jnp.sum(is_live.astype(jnp.int32))
    packed_limit = jnp.where(is_live, query_pos, -1)[order]
    attended_heads = [
        attend(
            queries[:, head][order], packed_limit, head_columns(all_both, head), all_pos, live_count
        )[restore]
        for head in range(local_heads)
    ]
    attended = jnp.concatenate(attended_heads, axis=1)
    out_width = w_out.shape[1]
    column_half = tok_index % 2
    after_gather = -(jnp.abs(all_both[0, 0]) * 0)
    own_half = lax.all_gather(
        lax.dynamic_slice_in_dim(w_out, column_half * (out_width // 2), out_width // 2, 1)
        + after_gather,
        "head",
        axis=0,
        tiled=True,
    )
    partner_pairs = [(i, i ^ 1) for i in range(tok_count)]
    slot_rows = lax.all_to_all(attended, "head", split_axis=0, concat_axis=1, tiled=True)
    partner_rows = lax.ppermute(slot_rows, "tok", partner_pairs)
    both_parts = jnp.dot(
        jnp.concatenate([slot_rows, partner_rows], axis=0), own_half, preferred_element_type=jnp.float32
    ).astype(jnp.bfloat16)
    mine = both_parts[:own_rows]
    other = lax.ppermute(both_parts[own_rows:], "tok", partner_pairs)
    update = jnp.where(
        column_half == 0,
        jnp.concatenate([mine, other], axis=1),
        jnp.concatenate([other, mine], axis=1),
    )
    own_slots = lax.dynamic_slice_in_dim(
        recomp_rows, (tok_index * head_count + head_index) * own_rows, own_rows
    )
    update = jnp.where((own_slots >= 0)[:, None], update, 0.0).astype(jnp.bfloat16)
    return (update, merged_keys, merged_values)


def solution(mesh):
    in_specs = (
        P(("tok", "head"), None),
        P(("tok", "head"), None),
        P(("tok", "head"), None),
        P(None, "head"),
        P(None, "head"),
        P(None, "head"),
        P("head", None),
        P(),
        P(),
        P(),
    )
    out_specs = (P(("tok", "head"), None), P("tok", "head"), P("tok", "head"))
    return jax.shard_map(local, mesh=mesh, in_specs=in_specs, out_specs=out_specs, check_vma=False)
```

```python
import functools

import jax
import jax.numpy as jnp
from jax import lax
from jax.sharding import PartitionSpec as P
from jax.experimental import pallas as pl
from jax.experimental.pallas import tpu as pltpu

HDIM = 128
CH = 16
CL = 1024


theta = 10000.0
epsilon = 1e-05
negative = -1e30
far_position = 1073741824
key_block = 1024


def rotate(values, angle_at):
    half_dim = values.shape[-1] // 2
    frequency = theta ** (-(jnp.arange(half_dim, dtype=jnp.float32) * (2.0 / values.shape[-1])))
    angles = angle_at.astype(jnp.float32)[:, None] * frequency[None, :]
    cosine = jnp.cos(angles)[:, None, :]
    sine_term = jnp.sin(angles)[:, None, :]
    first_half = values[..., :half_dim]
    second_half = values[..., half_dim:]
    return jnp.concatenate(
        [
            first_half * cosine - second_half * sine_term,
            second_half * cosine + first_half * sine_term,
        ],
        axis=-1,
    )


def layer_norm(hidden):
    values = hidden.astype(jnp.float32)
    center = values - jnp.mean(values, axis=-1, keepdims=True)
    spread = jnp.mean(center * center, axis=-1, keepdims=True)
    return (center * lax.rsqrt(spread + epsilon)).astype(jnp.bfloat16)


def new_positions(library, span_slot, span_start):
    span_index = library // CL
    span_ids = jnp.arange(CH, dtype=jnp.int32)
    slot_index = jnp.sum(
        jnp.where(span_index[:, None] == span_ids[None, :], span_slot[None, :], 0), axis=1
    )
    start_pos = jnp.sum(
        jnp.where(slot_index[:, None] == span_ids[None, :], span_start[None, :], 0), axis=1
    )
    return start_pos + library % CL


query_tile = 512
key_tile = 4096


def attention_kernel(
    low_limit, high_limit, low_pos, high_pos, q_ref, limit_ref, kv_ref, pos_ref, out_ref,
    peak_ref, total_ref, sum_ref,
):
    query_step = pl.program_id(0)
    key_step = pl.program_id(1)

    @pl.when(key_step == 0)
    def _():
        peak_ref[...] = jnp.full(peak_ref.shape, negative, jnp.float32)
        total_ref[...] = jnp.zeros(total_ref.shape, jnp.float32)
        sum_ref[...] = jnp.zeros(sum_ref.shape, jnp.float32)

    def absorb(masked):
        width = q_ref.shape[1]
        part_keys = kv_ref[:, :width]
        part_values = kv_ref[:, width:]
        scores = lax.dot_general(
            q_ref[...], part_keys, (((1,), (1,)), ((), ())), preferred_element_type=jnp.float32
        ) * (width ** -0.5)
        if masked:
            visible = pos_ref[...] <= limit_ref[...]
            scores = jnp.where(visible, scores, negative)
        old_peak = peak_ref[...]
        new_peak = jnp.maximum(old_peak, jnp.max(scores, axis=1, keepdims=True))
        factor = jnp.exp(old_peak - new_peak)
        weights = jnp.exp(scores - new_peak)
        if masked:
            weights = jnp.where(visible, weights, 0.0)
        total_ref[...] = total_ref[...] * factor + jnp.sum(weights, axis=1, keepdims=True)
        sum_ref[...] = sum_ref[...] * factor + jnp.dot(
            weights.astype(jnp.bfloat16), part_values, preferred_element_type=jnp.float32
        )
        peak_ref[...] = new_peak

    all_seen = high_pos[key_step] <= low_limit[query_step]
    none_seen = low_pos[key_step] > high_limit[query_step]

    @pl.when(all_seen)
    def _():
        absorb(False)

    @pl.when(jnp.logical_and(jnp.logical_not(all_seen), jnp.logical_not(none_seen)))
    def _():
        absorb(True)

    @pl.when(key_step == pl.num_programs(1) - 1)
    def _():
        out_ref[...] = (sum_ref[...] / total_ref[...]).astype(out_ref.dtype)


def attend(queries, query_limit, keys_values, key_pos):
    rows, width = queries.shape
    count = keys_values.shape[0]
    q_tile = min(query_tile, rows)
    k_tile = min(key_tile, count)
    tiled_limit = query_limit.reshape(rows // q_tile, q_tile)
    tiled_pos = key_pos.reshape(count // k_tile, k_tile)
    grid_spec = pltpu.PrefetchScalarGridSpec(
        num_scalar_prefetch=4,
        grid=(rows // q_tile, count // k_tile),
        in_specs=[
            pl.BlockSpec((q_tile, width), lambda i, j, *_: (i, 0)),
            pl.BlockSpec((q_tile, 1), lambda i, j, *_: (i, 0)),
            pl.BlockSpec((k_tile, 2 * width), lambda i, j, *_: (j, 0)),
            pl.BlockSpec((1, k_tile), lambda i, j, *_: (0, j)),
        ],
        out_specs=pl.BlockSpec((q_tile, width), lambda i, j, *_: (i, 0)),
        scratch_shapes=[
            pltpu.VMEM((q_tile, 1), jnp.float32),
            pltpu.VMEM((q_tile, 1), jnp.float32),
            pltpu.VMEM((q_tile, width), jnp.float32),
        ],
    )
    return pl.pallas_call(
        attention_kernel,
        grid_spec=grid_spec,
        out_shape=jax.ShapeDtypeStruct((rows, width), jnp.bfloat16),
        compiler_params=pltpu.CompilerParams(
            dimension_semantics=("arbitrary", "arbitrary"), vmem_limit_bytes=48 * 1024 * 1024
        ),
    )(
        jnp.min(tiled_limit, axis=1),
        jnp.max(tiled_limit, axis=1),
        jnp.min(tiled_pos, axis=1),
        jnp.max(tiled_pos, axis=1),
        queries,
        query_limit.reshape(rows, 1),
        keys_values,
        key_pos.reshape(1, count),
    )


def online_update(running, queries, query_limit, part_keys, part_values, part_pos):
    run_peak, run_total, run_sum = running
    scores = jnp.einsum(
        "qhd,khd->hqk", queries, part_keys, preferred_element_type=jnp.float32
    ) * HDIM ** (-0.5)
    visible = part_pos[None, None, :] <= query_limit[None, :, None]
    scores = jnp.where(visible, scores, negative)
    new_peak = jnp.maximum(run_peak, jnp.max(scores, axis=-1))
    factor = jnp.exp(run_peak - new_peak)
    weights = jnp.where(visible, jnp.exp(scores - new_peak[..., None]), 0.0)
    run_total = run_total * factor + jnp.sum(weights, axis=-1)
    added = jnp.einsum(
        "hqk,khd->hqd",
        weights.astype(jnp.bfloat16),
        part_values,
        preferred_element_type=jnp.float32,
    )
    run_sum = run_sum * factor[..., None] + added
    return (new_peak, run_total, run_sum)


def local(
    hidden_in,
    cache_keys,
    cache_values,
    w_query,
    w_key,
    w_value,
    w_out,
    span_slot,
    span_start,
    recomp_rows,
):
    head_count = lax.axis_size("head")
    tok_count = lax.axis_size("tok")
    tok_index = lax.axis_index("tok")
    head_index = lax.axis_index("head")
    own_rows = hidden_in.shape[0]
    head_width = w_query.shape[1]
    local_heads = head_width // HDIM
    group_rows = own_rows * head_count
    normed = layer_norm(hidden_in)
    w_joined = jnp.concatenate([w_query, w_key, w_value], axis=1)
    projected = jnp.dot(
        lax.all_gather(normed, "head", axis=0, tiled=True),
        w_joined,
        preferred_element_type=jnp.float32,
    )
    group_slots = lax.dynamic_slice_in_dim(recomp_rows, tok_index * group_rows, group_rows)
    is_live = group_slots >= 0
    query_pos = new_positions(jnp.maximum(group_slots, 0), span_slot, span_start)
    queries = rotate(
        projected[:, :head_width].reshape(group_rows, local_heads, HDIM), query_pos
    ).astype(jnp.bfloat16)
    fresh_keys = rotate(
        projected[:, head_width : 2 * head_width].reshape(group_rows, local_heads, HDIM), query_pos
    ).astype(jnp.bfloat16)
    fresh_values = (
        projected[:, 2 * head_width :].astype(jnp.bfloat16).reshape(group_rows, local_heads, HDIM)
    )
    moved_keys, moved_values = (
        lax.all_to_all(cache_keys, "head", split_axis=1, concat_axis=0, tiled=True),
        lax.all_to_all(cache_values, "head", split_axis=1, concat_axis=0, tiled=True),
    )
    block_len = moved_keys.shape[0]
    library = tok_index * block_len + jnp.arange(block_len, dtype=jnp.int32)
    key_pos = new_positions(library, span_slot, span_start)
    shifted = rotate(
        moved_keys.astype(jnp.float32).reshape(block_len, local_heads, HDIM), key_pos - library % CL
    ).astype(jnp.bfloat16)
    target = jnp.where(is_live, group_slots - tok_index * block_len, block_len)
    merged_keys = shifted.at[target].set(fresh_keys, mode="drop").reshape(block_len, head_width)
    merged_values = (
        moved_values.reshape(block_len, local_heads, HDIM)
        .at[target]
        .set(fresh_values, mode="drop")
        .reshape(block_len, head_width)
    )
    query_limit = jnp.where(is_live, query_pos, far_position)
    merged_both = jnp.concatenate([merged_keys, merged_values], axis=1)
    all_both = lax.all_gather(merged_both, "tok", axis=0, tiled=True)
    count_keys = all_both.shape[0]
    all_pos = new_positions(jnp.arange(count_keys, dtype=jnp.int32), span_slot, span_start)

    def head_columns(both, head):
        if local_heads == 1:
            return both
        return jnp.concatenate(
            [
                both[:, head * HDIM : (head + 1) * HDIM],
                both[:, head_width + head * HDIM : head_width + (head + 1) * HDIM],
            ],
            axis=1,
        )

    attended_heads = [
        attend(queries[:, head], query_limit, head_columns(all_both, head), all_pos)
        for head in range(local_heads)
    ]
    attended = jnp.concatenate(attended_heads, axis=1)
    out_width = w_out.shape[1]
    column_half = tok_index % 2
    after_gather = -(jnp.abs(all_both[0, 0]) * 0)
    own_half = lax.all_gather(
        lax.dynamic_slice_in_dim(w_out, column_half * (out_width // 2), out_width // 2, 1)
        + after_gather,
        "head",
        axis=0,
        tiled=True,
    )
    partner_pairs = [(i, i ^ 1) for i in range(tok_count)]
    slot_rows = lax.all_to_all(attended, "head", split_axis=0, concat_axis=1, tiled=True)
    partner_rows = lax.ppermute(slot_rows, "tok", partner_pairs)
    both_parts = jnp.dot(
        jnp.concatenate([slot_rows, partner_rows], axis=0), own_half, preferred_element_type=jnp.float32
    ).astype(jnp.bfloat16)
    mine = both_parts[:own_rows]
    other = lax.ppermute(both_parts[own_rows:], "tok", partner_pairs)
    update = jnp.where(
        column_half == 0,
        jnp.concatenate([mine, other], axis=1),
        jnp.concatenate([other, mine], axis=1),
    )
    own_slots = lax.dynamic_slice_in_dim(
        recomp_rows, (tok_index * head_count + head_index) * own_rows, own_rows
    )
    update = jnp.where((own_slots >= 0)[:, None], update, 0.0).astype(jnp.bfloat16)
    return (update, merged_keys, merged_values)


def solution(mesh):
    in_specs = (
        P(("tok", "head"), None),
        P(("tok", "head"), None),
        P(("tok", "head"), None),
        P(None, "head"),
        P(None, "head"),
        P(None, "head"),
        P("head", None),
        P(),
        P(),
        P(),
    )
    out_specs = (P(("tok", "head"), None), P("tok", "head"), P("tok", "head"))
    return jax.shard_map(local, mesh=mesh, in_specs=in_specs, out_specs=out_specs, check_vma=False)
```

```python
import functools

import jax
import jax.numpy as jnp
from jax import lax
from jax.sharding import PartitionSpec as P
from jax.experimental import pallas as pl
from jax.experimental.pallas import tpu as pltpu

HDIM = 128
CH = 16
CL = 1024


theta = 10000.0
epsilon = 1e-05
negative = -1e30
far_position = 1073741824
key_block = 1024


def rotate(values, angle_at):
    half_dim = values.shape[-1] // 2
    frequency = theta ** (-(jnp.arange(half_dim, dtype=jnp.float32) * (2.0 / values.shape[-1])))
    angles = angle_at.astype(jnp.float32)[:, None] * frequency[None, :]
    cosine = jnp.cos(angles)[:, None, :]
    sine_term = jnp.sin(angles)[:, None, :]
    first_half = values[..., :half_dim]
    second_half = values[..., half_dim:]
    return jnp.concatenate(
        [
            first_half * cosine - second_half * sine_term,
            second_half * cosine + first_half * sine_term,
        ],
        axis=-1,
    )


def layer_norm(hidden):
    values = hidden.astype(jnp.float32)
    center = values - jnp.mean(values, axis=-1, keepdims=True)
    spread = jnp.mean(center * center, axis=-1, keepdims=True)
    return (center * lax.rsqrt(spread + epsilon)).astype(jnp.bfloat16)


def new_positions(library, span_slot, span_start):
    span_index = library // CL
    span_ids = jnp.arange(CH, dtype=jnp.int32)
    slot_index = jnp.sum(
        jnp.where(span_index[:, None] == span_ids[None, :], span_slot[None, :], 0), axis=1
    )
    start_pos = jnp.sum(
        jnp.where(slot_index[:, None] == span_ids[None, :], span_start[None, :], 0), axis=1
    )
    return start_pos + library % CL


query_tile = 512
key_tile = 4096


def attention_kernel(
    low_limit, high_limit, low_pos, high_pos, q_ref, limit_ref, kv_ref, pos_ref, out_ref,
    peak_ref, total_ref, sum_ref,
):
    query_step = pl.program_id(0)
    key_step = pl.program_id(1)

    @pl.when(key_step == 0)
    def _():
        peak_ref[...] = jnp.full(peak_ref.shape, negative, jnp.float32)
        total_ref[...] = jnp.zeros(total_ref.shape, jnp.float32)
        sum_ref[...] = jnp.zeros(sum_ref.shape, jnp.float32)

    def absorb(masked):
        width = q_ref.shape[1]
        part_keys = kv_ref[:, :width]
        part_values = kv_ref[:, width:]
        scores = lax.dot_general(
            q_ref[...], part_keys, (((1,), (1,)), ((), ())), preferred_element_type=jnp.float32
        ) * (width ** -0.5)
        if masked:
            visible = pos_ref[...] <= limit_ref[...]
            scores = jnp.where(visible, scores, negative)
        old_peak = peak_ref[...]
        new_peak = jnp.maximum(old_peak, jnp.max(scores, axis=1, keepdims=True))
        factor = jnp.exp(old_peak - new_peak)
        weights = jnp.exp(scores - new_peak)
        if masked:
            weights = jnp.where(visible, weights, 0.0)
        total_ref[...] = total_ref[...] * factor + jnp.sum(weights, axis=1, keepdims=True)
        sum_ref[...] = sum_ref[...] * factor + jnp.dot(
            weights.astype(jnp.bfloat16), part_values, preferred_element_type=jnp.float32
        )
        peak_ref[...] = new_peak

    all_seen = high_pos[key_step] <= low_limit[query_step]
    none_seen = low_pos[key_step] > high_limit[query_step]

    @pl.when(all_seen)
    def _():
        absorb(False)

    @pl.when(jnp.logical_and(jnp.logical_not(all_seen), jnp.logical_not(none_seen)))
    def _():
        absorb(True)

    @pl.when(key_step == pl.num_programs(1) - 1)
    def _():
        out_ref[...] = (sum_ref[...] / total_ref[...]).astype(out_ref.dtype)


def attend(queries, query_limit, keys_values, key_pos):
    rows, width = queries.shape
    count = keys_values.shape[0]
    q_tile = min(query_tile, rows)
    k_tile = min(key_tile, count)
    tiled_limit = query_limit.reshape(rows // q_tile, q_tile)
    tiled_pos = key_pos.reshape(count // k_tile, k_tile)
    grid_spec = pltpu.PrefetchScalarGridSpec(
        num_scalar_prefetch=4,
        grid=(rows // q_tile, count // k_tile),
        in_specs=[
            pl.BlockSpec((q_tile, width), lambda i, j, *_: (i, 0)),
            pl.BlockSpec((q_tile, 1), lambda i, j, *_: (i, 0)),
            pl.BlockSpec((k_tile, 2 * width), lambda i, j, *_: (j, 0)),
            pl.BlockSpec((1, k_tile), lambda i, j, *_: (0, j)),
        ],
        out_specs=pl.BlockSpec((q_tile, width), lambda i, j, *_: (i, 0)),
        scratch_shapes=[
            pltpu.VMEM((q_tile, 1), jnp.float32),
            pltpu.VMEM((q_tile, 1), jnp.float32),
            pltpu.VMEM((q_tile, width), jnp.float32),
        ],
    )
    return pl.pallas_call(
        attention_kernel,
        grid_spec=grid_spec,
        out_shape=jax.ShapeDtypeStruct((rows, width), jnp.bfloat16),
        compiler_params=pltpu.CompilerParams(
            dimension_semantics=("arbitrary", "arbitrary"), vmem_limit_bytes=48 * 1024 * 1024
        ),
    )(
        jnp.min(tiled_limit, axis=1),
        jnp.max(tiled_limit, axis=1),
        jnp.min(tiled_pos, axis=1),
        jnp.max(tiled_pos, axis=1),
        queries,
        query_limit.reshape(rows, 1),
        keys_values,
        key_pos.reshape(1, count),
    )


def online_update(running, queries, query_limit, part_keys, part_values, part_pos):
    run_peak, run_total, run_sum = running
    scores = jnp.einsum(
        "qhd,khd->hqk", queries, part_keys, preferred_element_type=jnp.float32
    ) * HDIM ** (-0.5)
    visible = part_pos[None, None, :] <= query_limit[None, :, None]
    scores = jnp.where(visible, scores, negative)
    new_peak = jnp.maximum(run_peak, jnp.max(scores, axis=-1))
    factor = jnp.exp(run_peak - new_peak)
    weights = jnp.where(visible, jnp.exp(scores - new_peak[..., None]), 0.0)
    run_total = run_total * factor + jnp.sum(weights, axis=-1)
    added = jnp.einsum(
        "hqk,khd->hqd",
        weights.astype(jnp.bfloat16),
        part_values,
        preferred_element_type=jnp.float32,
    )
    run_sum = run_sum * factor[..., None] + added
    return (new_peak, run_total, run_sum)


def local(
    hidden_in,
    cache_keys,
    cache_values,
    w_query,
    w_key,
    w_value,
    w_out,
    span_slot,
    span_start,
    recomp_rows,
):
    head_count = lax.axis_size("head")
    tok_count = lax.axis_size("tok")
    tok_index = lax.axis_index("tok")
    head_index = lax.axis_index("head")
    own_rows = hidden_in.shape[0]
    head_width = w_query.shape[1]
    local_heads = head_width // HDIM
    group_rows = own_rows * head_count
    normed = layer_norm(hidden_in)
    w_joined = jnp.concatenate([w_query, w_key, w_value], axis=1)
    projected = jnp.dot(
        lax.all_gather(normed, "head", axis=0, tiled=True),
        w_joined,
        preferred_element_type=jnp.float32,
    )
    group_slots = lax.dynamic_slice_in_dim(recomp_rows, tok_index * group_rows, group_rows)
    is_live = group_slots >= 0
    query_pos = new_positions(jnp.maximum(group_slots, 0), span_slot, span_start)
    queries = rotate(
        projected[:, :head_width].reshape(group_rows, local_heads, HDIM), query_pos
    ).astype(jnp.bfloat16)
    fresh_keys = rotate(
        projected[:, head_width : 2 * head_width].reshape(group_rows, local_heads, HDIM), query_pos
    ).astype(jnp.bfloat16)
    fresh_values = (
        projected[:, 2 * head_width :].astype(jnp.bfloat16).reshape(group_rows, local_heads, HDIM)
    )
    moved_keys, moved_values = (
        lax.all_to_all(cache_keys, "head", split_axis=1, concat_axis=0, tiled=True),
        lax.all_to_all(cache_values, "head", split_axis=1, concat_axis=0, tiled=True),
    )
    block_len = moved_keys.shape[0]
    library = tok_index * block_len + jnp.arange(block_len, dtype=jnp.int32)
    key_pos = new_positions(library, span_slot, span_start)
    shifted = rotate(
        moved_keys.astype(jnp.float32).reshape(block_len, local_heads, HDIM), key_pos - library % CL
    ).astype(jnp.bfloat16)
    target = jnp.where(is_live, group_slots - tok_index * block_len, block_len)
    picks = jnp.arange(block_len, dtype=jnp.int32)[:, None] == target[None, :]
    fresh_both = jnp.concatenate(
        [fresh_keys.reshape(group_rows, head_width), fresh_values.reshape(group_rows, head_width)], axis=1
    )
    picked = jnp.dot(
        picks.astype(jnp.bfloat16), fresh_both, preferred_element_type=jnp.float32
    ).astype(jnp.bfloat16)
    replaced = jnp.any(picks, axis=1)[:, None]
    merged_both = jnp.where(
        replaced,
        picked,
        jnp.concatenate([shifted.reshape(block_len, head_width), moved_values], axis=1),
    )
    merged_keys = merged_both[:, :head_width]
    merged_values = merged_both[:, head_width:]
    query_limit = jnp.where(is_live, query_pos, far_position)
    all_both = lax.all_gather(merged_both, "tok", axis=0, tiled=True)
    count_keys = all_both.shape[0]
    all_pos = new_positions(jnp.arange(count_keys, dtype=jnp.int32), span_slot, span_start)

    def head_columns(both, head):
        if local_heads == 1:
            return both
        return jnp.concatenate(
            [
                both[:, head * HDIM : (head + 1) * HDIM],
                both[:, head_width + head * HDIM : head_width + (head + 1) * HDIM],
            ],
            axis=1,
        )

    attended_heads = [
        attend(queries[:, head], query_limit, head_columns(all_both, head), all_pos)
        for head in range(local_heads)
    ]
    attended = jnp.concatenate(attended_heads, axis=1)
    out_width = w_out.shape[1]
    column_half = tok_index % 2
    after_gather = -(jnp.abs(all_both[0, 0]) * 0)
    own_half = lax.all_gather(
        lax.dynamic_slice_in_dim(w_out, column_half * (out_width // 2), out_width // 2, 1)
        + after_gather,
        "head",
        axis=0,
        tiled=True,
    )
    partner_pairs = [(i, i ^ 1) for i in range(tok_count)]
    slot_rows = lax.all_to_all(attended, "head", split_axis=0, concat_axis=1, tiled=True)
    partner_rows = lax.ppermute(slot_rows, "tok", partner_pairs)
    both_parts = jnp.dot(
        jnp.concatenate([slot_rows, partner_rows], axis=0), own_half, preferred_element_type=jnp.float32
    ).astype(jnp.bfloat16)
    mine = both_parts[:own_rows]
    other = lax.ppermute(both_parts[own_rows:], "tok", partner_pairs)
    update = jnp.where(
        column_half == 0,
        jnp.concatenate([mine, other], axis=1),
        jnp.concatenate([other, mine], axis=1),
    )
    own_slots = lax.dynamic_slice_in_dim(
        recomp_rows, (tok_index * head_count + head_index) * own_rows, own_rows
    )
    update = jnp.where((own_slots >= 0)[:, None], update, 0.0).astype(jnp.bfloat16)
    return (update, merged_keys, merged_values)


def solution(mesh):
    in_specs = (
        P(("tok", "head"), None),
        P(("tok", "head"), None),
        P(("tok", "head"), None),
        P(None, "head"),
        P(None, "head"),
        P(None, "head"),
        P("head", None),
        P(),
        P(),
        P(),
    )
    out_specs = (P(("tok", "head"), None), P("tok", "head"), P("tok", "head"))
    return jax.shard_map(local, mesh=mesh, in_specs=in_specs, out_specs=out_specs, check_vma=False)
```

```python
import functools

import jax
import jax.numpy as jnp
from jax import lax
from jax.sharding import PartitionSpec as P
from jax.experimental import pallas as pl
from jax.experimental.pallas import tpu as pltpu

HDIM = 128
CH = 16
CL = 1024


theta = 10000.0
epsilon = 1e-05
negative = -1e30
far_position = 1073741824
key_block = 1024


def rotate(values, angle_at):
    half_dim = values.shape[-1] // 2
    frequency = theta ** (-(jnp.arange(half_dim, dtype=jnp.float32) * (2.0 / values.shape[-1])))
    angles = angle_at.astype(jnp.float32)[:, None] * frequency[None, :]
    cosine = jnp.cos(angles)[:, None, :]
    sine_term = jnp.sin(angles)[:, None, :]
    first_half = values[..., :half_dim]
    second_half = values[..., half_dim:]
    return jnp.concatenate(
        [
            first_half * cosine - second_half * sine_term,
            second_half * cosine + first_half * sine_term,
        ],
        axis=-1,
    )


def layer_norm(hidden):
    values = hidden.astype(jnp.float32)
    center = values - jnp.mean(values, axis=-1, keepdims=True)
    spread = jnp.mean(center * center, axis=-1, keepdims=True)
    return (center * lax.rsqrt(spread + epsilon)).astype(jnp.bfloat16)


def new_positions(library, span_slot, span_start):
    span_index = library // CL
    span_ids = jnp.arange(CH, dtype=jnp.int32)
    slot_index = jnp.sum(
        jnp.where(span_index[:, None] == span_ids[None, :], span_slot[None, :], 0), axis=1
    )
    start_pos = jnp.sum(
        jnp.where(slot_index[:, None] == span_ids[None, :], span_start[None, :], 0), axis=1
    )
    return start_pos + library % CL


query_tile = 512
key_tile = 4096


def attention_kernel(
    low_limit, high_limit, low_pos, high_pos, q_ref, limit_ref, kv_ref, pos_ref, out_ref,
    peak_ref, total_ref, sum_ref,
):
    query_step = pl.program_id(0)
    key_step = pl.program_id(1)

    @pl.when(key_step == 0)
    def _():
        peak_ref[...] = jnp.full(peak_ref.shape, negative, jnp.float32)
        total_ref[...] = jnp.zeros(total_ref.shape, jnp.float32)
        sum_ref[...] = jnp.zeros(sum_ref.shape, jnp.float32)

    def absorb(masked):
        width = q_ref.shape[1]
        part_keys = kv_ref[:, :width]
        part_values = kv_ref[:, width:]
        scores = lax.dot_general(
            q_ref[...], part_keys, (((1,), (1,)), ((), ())), preferred_element_type=jnp.float32
        ) * (width ** -0.5)
        if masked:
            visible = pos_ref[...] <= limit_ref[...]
            scores = jnp.where(visible, scores, negative)
        old_peak = peak_ref[...]
        new_peak = jnp.maximum(old_peak, jnp.max(scores, axis=1, keepdims=True))
        factor = jnp.exp(old_peak - new_peak)
        weights = jnp.exp(scores - new_peak)
        if masked:
            weights = jnp.where(visible, weights, 0.0)
        total_ref[...] = total_ref[...] * factor + jnp.sum(weights, axis=1, keepdims=True)
        sum_ref[...] = sum_ref[...] * factor + jnp.dot(
            weights.astype(jnp.bfloat16), part_values, preferred_element_type=jnp.float32
        )
        peak_ref[...] = new_peak

    all_seen = high_pos[key_step] <= low_limit[query_step]
    none_seen = low_pos[key_step] > high_limit[query_step]

    @pl.when(all_seen)
    def _():
        absorb(False)

    @pl.when(jnp.logical_and(jnp.logical_not(all_seen), jnp.logical_not(none_seen)))
    def _():
        absorb(True)

    @pl.when(key_step == pl.num_programs(1) - 1)
    def _():
        out_ref[...] = (sum_ref[...] / total_ref[...]).astype(out_ref.dtype)


def tile_bounds(query_limit, key_pos):
    rows = query_limit.shape[0]
    count = key_pos.shape[0]
    tiled_limit = query_limit.reshape(rows // min(query_tile, rows), -1)
    tiled_pos = key_pos.reshape(count // min(key_tile, count), -1)
    return (
        jnp.min(tiled_limit, axis=1),
        jnp.max(tiled_limit, axis=1),
        jnp.min(tiled_pos, axis=1),
        jnp.max(tiled_pos, axis=1),
    )


def attend(queries, query_limit, keys_values, key_pos, bounds):
    rows, width = queries.shape
    count = keys_values.shape[0]
    q_tile = min(query_tile, rows)
    k_tile = min(key_tile, count)
    grid_spec = pltpu.PrefetchScalarGridSpec(
        num_scalar_prefetch=4,
        grid=(rows // q_tile, count // k_tile),
        in_specs=[
            pl.BlockSpec((q_tile, width), lambda i, j, *_: (i, 0)),
            pl.BlockSpec((q_tile, 1), lambda i, j, *_: (i, 0)),
            pl.BlockSpec((k_tile, 2 * width), lambda i, j, *_: (j, 0)),
            pl.BlockSpec((1, k_tile), lambda i, j, *_: (0, j)),
        ],
        out_specs=pl.BlockSpec((q_tile, width), lambda i, j, *_: (i, 0)),
        scratch_shapes=[
            pltpu.VMEM((q_tile, 1), jnp.float32),
            pltpu.VMEM((q_tile, 1), jnp.float32),
            pltpu.VMEM((q_tile, width), jnp.float32),
        ],
    )
    return pl.pallas_call(
        attention_kernel,
        grid_spec=grid_spec,
        out_shape=jax.ShapeDtypeStruct((rows, width), jnp.bfloat16),
        compiler_params=pltpu.CompilerParams(
            dimension_semantics=("arbitrary", "arbitrary"), vmem_limit_bytes=48 * 1024 * 1024
        ),
    )(
        *bounds,
        queries,
        query_limit.reshape(rows, 1),
        keys_values,
        key_pos.reshape(1, count),
    )


def online_update(running, queries, query_limit, part_keys, part_values, part_pos):
    run_peak, run_total, run_sum = running
    scores = jnp.einsum(
        "qhd,khd->hqk", queries, part_keys, preferred_element_type=jnp.float32
    ) * HDIM ** (-0.5)
    visible = part_pos[None, None, :] <= query_limit[None, :, None]
    scores = jnp.where(visible, scores, negative)
    new_peak = jnp.maximum(run_peak, jnp.max(scores, axis=-1))
    factor = jnp.exp(run_peak - new_peak)
    weights = jnp.where(visible, jnp.exp(scores - new_peak[..., None]), 0.0)
    run_total = run_total * factor + jnp.sum(weights, axis=-1)
    added = jnp.einsum(
        "hqk,khd->hqd",
        weights.astype(jnp.bfloat16),
        part_values,
        preferred_element_type=jnp.float32,
    )
    run_sum = run_sum * factor[..., None] + added
    return (new_peak, run_total, run_sum)


def local(
    hidden_in,
    cache_keys,
    cache_values,
    w_query,
    w_key,
    w_value,
    w_out,
    span_slot,
    span_start,
    recomp_rows,
):
    head_count = lax.axis_size("head")
    tok_count = lax.axis_size("tok")
    tok_index = lax.axis_index("tok")
    head_index = lax.axis_index("head")
    own_rows = hidden_in.shape[0]
    head_width = w_query.shape[1]
    local_heads = head_width // HDIM
    group_rows = own_rows * head_count
    normed = layer_norm(hidden_in)
    group_slots = lax.dynamic_slice_in_dim(recomp_rows, tok_index * group_rows, group_rows)
    is_live = group_slots >= 0
    query_pos = new_positions(jnp.maximum(group_slots, 0), span_slot, span_start)
    query_limit = jnp.where(is_live, query_pos, far_position)
    count_keys = cache_keys.shape[0] * head_count * tok_count
    all_pos = new_positions(jnp.arange(count_keys, dtype=jnp.int32), span_slot, span_start)
    bounds = tile_bounds(query_limit, all_pos)
    after_bounds = -(jnp.abs(sum(bound[0] for bound in bounds).astype(jnp.bfloat16)) * 0)
    w_joined = jnp.concatenate([w_query, w_key, w_value], axis=1) + after_bounds
    projected = jnp.dot(
        lax.all_gather(normed, "head", axis=0, tiled=True),
        w_joined,
        preferred_element_type=jnp.float32,
    )
    queries = rotate(
        projected[:, :head_width].reshape(group_rows, local_heads, HDIM), query_pos
    ).astype(jnp.bfloat16)
    fresh_keys = rotate(
        projected[:, head_width : 2 * head_width].reshape(group_rows, local_heads, HDIM), query_pos
    ).astype(jnp.bfloat16)
    fresh_values = (
        projected[:, 2 * head_width :].astype(jnp.bfloat16).reshape(group_rows, local_heads, HDIM)
    )
    moved_keys, moved_values = (
        lax.all_to_all(cache_keys, "head", split_axis=1, concat_axis=0, tiled=True),
        lax.all_to_all(cache_values, "head", split_axis=1, concat_axis=0, tiled=True),
    )
    block_len = moved_keys.shape[0]
    library = tok_index * block_len + jnp.arange(block_len, dtype=jnp.int32)
    key_pos = new_positions(library, span_slot, span_start)
    shifted = rotate(
        moved_keys.astype(jnp.float32).reshape(block_len, local_heads, HDIM), key_pos - library % CL
    ).astype(jnp.bfloat16)
    target = jnp.where(is_live, group_slots - tok_index * block_len, block_len)
    picks = jnp.arange(block_len, dtype=jnp.int32)[:, None] == target[None, :]
    fresh_both = jnp.concatenate(
        [fresh_keys.reshape(group_rows, head_width), fresh_values.reshape(group_rows, head_width)], axis=1
    )
    picked = jnp.dot(
        picks.astype(jnp.bfloat16), fresh_both, preferred_element_type=jnp.float32
    ).astype(jnp.bfloat16)
    replaced = jnp.any(picks, axis=1)[:, None]
    merged_both = jnp.where(
        replaced,
        picked,
        jnp.concatenate([shifted.reshape(block_len, head_width), moved_values], axis=1),
    )
    merged_keys = merged_both[:, :head_width]
    merged_values = merged_both[:, head_width:]
    all_both = lax.all_gather(merged_both, "tok", axis=0, tiled=True)

    def head_columns(both, head):
        if local_heads == 1:
            return both
        return jnp.concatenate(
            [
                both[:, head * HDIM : (head + 1) * HDIM],
                both[:, head_width + head * HDIM : head_width + (head + 1) * HDIM],
            ],
            axis=1,
        )

    attended_heads = [
        attend(queries[:, head], query_limit, head_columns(all_both, head), all_pos, bounds)
        for head in range(local_heads)
    ]
    attended = jnp.concatenate(attended_heads, axis=1)
    out_width = w_out.shape[1]
    column_half = tok_index % 2
    after_gather = -(jnp.abs(all_both[0, 0]) * 0)
    own_half = lax.all_gather(
        lax.dynamic_slice_in_dim(w_out, column_half * (out_width // 2), out_width // 2, 1)
        + after_gather,
        "head",
        axis=0,
        tiled=True,
    )
    partner_pairs = [(i, i ^ 1) for i in range(tok_count)]
    slot_rows = lax.all_to_all(attended, "head", split_axis=0, concat_axis=1, tiled=True)
    partner_rows = lax.ppermute(slot_rows, "tok", partner_pairs)
    both_parts = jnp.dot(
        jnp.concatenate([slot_rows, partner_rows], axis=0), own_half, preferred_element_type=jnp.float32
    ).astype(jnp.bfloat16)
    mine = both_parts[:own_rows]
    other = lax.ppermute(both_parts[own_rows:], "tok", partner_pairs)
    update = jnp.where(
        column_half == 0,
        jnp.concatenate([mine, other], axis=1),
        jnp.concatenate([other, mine], axis=1),
    )
    own_slots = lax.dynamic_slice_in_dim(
        recomp_rows, (tok_index * head_count + head_index) * own_rows, own_rows
    )
    update = jnp.where((own_slots >= 0)[:, None], update, 0.0).astype(jnp.bfloat16)
    return (update, merged_keys, merged_values)


def solution(mesh):
    in_specs = (
        P(("tok", "head"), None),
        P(("tok", "head"), None),
        P(("tok", "head"), None),
        P(None, "head"),
        P(None, "head"),
        P(None, "head"),
        P("head", None),
        P(),
        P(),
        P(),
    )
    out_specs = (P(("tok", "head"), None), P("tok", "head"), P("tok", "head"))
    return jax.shard_map(local, mesh=mesh, in_specs=in_specs, out_specs=out_specs, check_vma=False)
```

```python
import functools

import jax
import jax.numpy as jnp
from jax import lax
from jax.sharding import PartitionSpec as P
from jax.experimental import pallas as pl
from jax.experimental.pallas import tpu as pltpu

HDIM = 128
CH = 16
CL = 1024


theta = 10000.0
epsilon = 1e-05
negative = -1e30
far_position = 1073741824
key_block = 1024


def rotate(values, angle_at):
    half_dim = values.shape[-1] // 2
    frequency = theta ** (-(jnp.arange(half_dim, dtype=jnp.float32) * (2.0 / values.shape[-1])))
    angles = angle_at.astype(jnp.float32)[:, None] * frequency[None, :]
    cosine = jnp.cos(angles)[:, None, :]
    sine_term = jnp.sin(angles)[:, None, :]
    first_half = values[..., :half_dim]
    second_half = values[..., half_dim:]
    return jnp.concatenate(
        [
            first_half * cosine - second_half * sine_term,
            second_half * cosine + first_half * sine_term,
        ],
        axis=-1,
    )


def layer_norm(hidden):
    values = hidden.astype(jnp.float32)
    center = values - jnp.mean(values, axis=-1, keepdims=True)
    spread = jnp.mean(center * center, axis=-1, keepdims=True)
    return (center * lax.rsqrt(spread + epsilon)).astype(jnp.bfloat16)


def new_positions(library, span_slot, span_start):
    span_index = library // CL
    span_ids = jnp.arange(CH, dtype=jnp.int32)
    slot_index = jnp.sum(
        jnp.where(span_index[:, None] == span_ids[None, :], span_slot[None, :], 0), axis=1
    )
    start_pos = jnp.sum(
        jnp.where(slot_index[:, None] == span_ids[None, :], span_start[None, :], 0), axis=1
    )
    return start_pos + library % CL


query_tile = 512
log2_e = 1.4426950408889634
key_tile = 4096


def attention_kernel(
    low_limit, high_limit, low_pos, high_pos, q_ref, limit_ref, kv_ref, pos_ref, out_ref,
    peak_ref, total_ref, sum_ref,
):
    query_step = pl.program_id(0)
    key_step = pl.program_id(1)

    @pl.when(key_step == 0)
    def _():
        peak_ref[...] = jnp.full(peak_ref.shape, negative, jnp.float32)
        total_ref[...] = jnp.zeros(total_ref.shape, jnp.float32)
        sum_ref[...] = jnp.zeros(sum_ref.shape, jnp.float32)

    def absorb(masked):
        width = q_ref.shape[1]
        part_keys = kv_ref[:, :width]
        part_values = kv_ref[:, width:]
        scores = lax.dot_general(
            q_ref[...], part_keys, (((1,), (1,)), ((), ())), preferred_element_type=jnp.float32
        ) * (width ** -0.5 * log2_e)
        if masked:
            visible = pos_ref[...] <= limit_ref[...]
            scores = jnp.where(visible, scores, negative)
        old_peak = peak_ref[...]
        new_peak = jnp.maximum(old_peak, jnp.max(scores, axis=1, keepdims=True))
        factor = jnp.exp2(old_peak - new_peak)
        weights = jnp.exp2(scores - new_peak)
        if masked:
            weights = jnp.where(visible, weights, 0.0)
        total_ref[...] = total_ref[...] * factor + jnp.sum(weights, axis=1, keepdims=True)
        sum_ref[...] = sum_ref[...] * factor + jnp.dot(
            weights.astype(jnp.bfloat16), part_values, preferred_element_type=jnp.float32
        )
        peak_ref[...] = new_peak

    all_seen = high_pos[key_step] <= low_limit[query_step]
    none_seen = low_pos[key_step] > high_limit[query_step]

    @pl.when(all_seen)
    def _():
        absorb(False)

    @pl.when(jnp.logical_and(jnp.logical_not(all_seen), jnp.logical_not(none_seen)))
    def _():
        absorb(True)

    @pl.when(key_step == pl.num_programs(1) - 1)
    def _():
        out_ref[...] = (sum_ref[...] / total_ref[...]).astype(out_ref.dtype)


def tile_bounds(query_limit, key_pos):
    rows = query_limit.shape[0]
    count = key_pos.shape[0]
    tiled_limit = query_limit.reshape(rows // min(query_tile, rows), -1)
    tiled_pos = key_pos.reshape(count // min(key_tile, count), -1)
    return (
        jnp.min(tiled_limit, axis=1),
        jnp.max(tiled_limit, axis=1),
        jnp.min(tiled_pos, axis=1),
        jnp.max(tiled_pos, axis=1),
    )


def attend(queries, query_limit, keys_values, key_pos, bounds):
    rows, width = queries.shape
    count = keys_values.shape[0]
    q_tile = min(query_tile, rows)
    k_tile = min(key_tile, count)
    grid_spec = pltpu.PrefetchScalarGridSpec(
        num_scalar_prefetch=4,
        grid=(rows // q_tile, count // k_tile),
        in_specs=[
            pl.BlockSpec((q_tile, width), lambda i, j, *_: (i, 0)),
            pl.BlockSpec((q_tile, 1), lambda i, j, *_: (i, 0)),
            pl.BlockSpec((k_tile, 2 * width), lambda i, j, *_: (j, 0)),
            pl.BlockSpec((1, k_tile), lambda i, j, *_: (0, j)),
        ],
        out_specs=pl.BlockSpec((q_tile, width), lambda i, j, *_: (i, 0)),
        scratch_shapes=[
            pltpu.VMEM((q_tile, 1), jnp.float32),
            pltpu.VMEM((q_tile, 1), jnp.float32),
            pltpu.VMEM((q_tile, width), jnp.float32),
        ],
    )
    return pl.pallas_call(
        attention_kernel,
        grid_spec=grid_spec,
        out_shape=jax.ShapeDtypeStruct((rows, width), jnp.bfloat16),
        compiler_params=pltpu.CompilerParams(
            dimension_semantics=("arbitrary", "arbitrary"), vmem_limit_bytes=48 * 1024 * 1024
        ),
    )(
        *bounds,
        queries,
        query_limit.reshape(rows, 1),
        keys_values,
        key_pos.reshape(1, count),
    )


def online_update(running, queries, query_limit, part_keys, part_values, part_pos):
    run_peak, run_total, run_sum = running
    scores = jnp.einsum(
        "qhd,khd->hqk", queries, part_keys, preferred_element_type=jnp.float32
    ) * HDIM ** (-0.5)
    visible = part_pos[None, None, :] <= query_limit[None, :, None]
    scores = jnp.where(visible, scores, negative)
    new_peak = jnp.maximum(run_peak, jnp.max(scores, axis=-1))
    factor = jnp.exp(run_peak - new_peak)
    weights = jnp.where(visible, jnp.exp(scores - new_peak[..., None]), 0.0)
    run_total = run_total * factor + jnp.sum(weights, axis=-1)
    added = jnp.einsum(
        "hqk,khd->hqd",
        weights.astype(jnp.bfloat16),
        part_values,
        preferred_element_type=jnp.float32,
    )
    run_sum = run_sum * factor[..., None] + added
    return (new_peak, run_total, run_sum)


def local(
    hidden_in,
    cache_keys,
    cache_values,
    w_query,
    w_key,
    w_value,
    w_out,
    span_slot,
    span_start,
    recomp_rows,
):
    head_count = lax.axis_size("head")
    tok_count = lax.axis_size("tok")
    tok_index = lax.axis_index("tok")
    head_index = lax.axis_index("head")
    own_rows = hidden_in.shape[0]
    head_width = w_query.shape[1]
    local_heads = head_width // HDIM
    group_rows = own_rows * head_count
    normed = layer_norm(hidden_in)
    group_slots = lax.dynamic_slice_in_dim(recomp_rows, tok_index * group_rows, group_rows)
    is_live = group_slots >= 0
    query_pos = new_positions(jnp.maximum(group_slots, 0), span_slot, span_start)
    query_limit = jnp.where(is_live, query_pos, far_position)
    count_keys = cache_keys.shape[0] * head_count * tok_count
    all_pos = new_positions(jnp.arange(count_keys, dtype=jnp.int32), span_slot, span_start)
    bounds = tile_bounds(query_limit, all_pos)
    after_bounds = -(jnp.abs(sum(bound[0] for bound in bounds).astype(jnp.bfloat16)) * 0)
    w_joined = jnp.concatenate([w_query, w_key, w_value], axis=1) + after_bounds
    projected = jnp.dot(
        lax.all_gather(normed, "head", axis=0, tiled=True),
        w_joined,
        preferred_element_type=jnp.float32,
    )
    queries = rotate(
        projected[:, :head_width].reshape(group_rows, local_heads, HDIM), query_pos
    ).astype(jnp.bfloat16)
    fresh_keys = rotate(
        projected[:, head_width : 2 * head_width].reshape(group_rows, local_heads, HDIM), query_pos
    ).astype(jnp.bfloat16)
    fresh_values = (
        projected[:, 2 * head_width :].astype(jnp.bfloat16).reshape(group_rows, local_heads, HDIM)
    )
    moved_keys, moved_values = (
        lax.all_to_all(cache_keys, "head", split_axis=1, concat_axis=0, tiled=True),
        lax.all_to_all(cache_values, "head", split_axis=1, concat_axis=0, tiled=True),
    )
    block_len = moved_keys.shape[0]
    library = tok_index * block_len + jnp.arange(block_len, dtype=jnp.int32)
    key_pos = new_positions(library, span_slot, span_start)
    shifted = rotate(
        moved_keys.astype(jnp.float32).reshape(block_len, local_heads, HDIM), key_pos - library % CL
    ).astype(jnp.bfloat16)
    target = jnp.where(is_live, group_slots - tok_index * block_len, block_len)
    picks = jnp.arange(block_len, dtype=jnp.int32)[:, None] == target[None, :]
    fresh_both = jnp.concatenate(
        [fresh_keys.reshape(group_rows, head_width), fresh_values.reshape(group_rows, head_width)], axis=1
    )
    picked = jnp.dot(
        picks.astype(jnp.bfloat16), fresh_both, preferred_element_type=jnp.float32
    ).astype(jnp.bfloat16)
    replaced = jnp.any(picks, axis=1)[:, None]
    merged_both = jnp.where(
        replaced,
        picked,
        jnp.concatenate([shifted.reshape(block_len, head_width), moved_values], axis=1),
    )
    merged_keys = merged_both[:, :head_width]
    merged_values = merged_both[:, head_width:]
    all_both = lax.all_gather(merged_both, "tok", axis=0, tiled=True)

    def head_columns(both, head):
        if local_heads == 1:
            return both
        return jnp.concatenate(
            [
                both[:, head * HDIM : (head + 1) * HDIM],
                both[:, head_width + head * HDIM : head_width + (head + 1) * HDIM],
            ],
            axis=1,
        )

    attended_heads = [
        attend(queries[:, head], query_limit, head_columns(all_both, head), all_pos, bounds)
        for head in range(local_heads)
    ]
    attended = jnp.concatenate(attended_heads, axis=1)
    out_width = w_out.shape[1]
    column_half = tok_index % 2
    after_gather = -(jnp.abs(all_both[0, 0]) * 0)
    own_half = lax.all_gather(
        lax.dynamic_slice_in_dim(w_out, column_half * (out_width // 2), out_width // 2, 1)
        + after_gather,
        "head",
        axis=0,
        tiled=True,
    )
    partner_pairs = [(i, i ^ 1) for i in range(tok_count)]
    slot_rows = lax.all_to_all(attended, "head", split_axis=0, concat_axis=1, tiled=True)
    partner_rows = lax.ppermute(slot_rows, "tok", partner_pairs)
    both_parts = jnp.dot(
        jnp.concatenate([slot_rows, partner_rows], axis=0), own_half, preferred_element_type=jnp.float32
    ).astype(jnp.bfloat16)
    mine = both_parts[:own_rows]
    other = lax.ppermute(both_parts[own_rows:], "tok", partner_pairs)
    update = jnp.where(
        column_half == 0,
        jnp.concatenate([mine, other], axis=1),
        jnp.concatenate([other, mine], axis=1),
    )
    own_slots = lax.dynamic_slice_in_dim(
        recomp_rows, (tok_index * head_count + head_index) * own_rows, own_rows
    )
    update = jnp.where((own_slots >= 0)[:, None], update, 0.0).astype(jnp.bfloat16)
    return (update, merged_keys, merged_values)


def solution(mesh):
    in_specs = (
        P(("tok", "head"), None),
        P(("tok", "head"), None),
        P(("tok", "head"), None),
        P(None, "head"),
        P(None, "head"),
        P(None, "head"),
        P("head", None),
        P(),
        P(),
        P(),
    )
    out_specs = (P(("tok", "head"), None), P("tok", "head"), P("tok", "head"))
    return jax.shard_map(local, mesh=mesh, in_specs=in_specs, out_specs=out_specs, check_vma=False)
```

```python
import functools

import jax
import jax.numpy as jnp
from jax import lax
from jax.sharding import PartitionSpec as P
from jax.experimental import pallas as pl
from jax.experimental.pallas import tpu as pltpu

HDIM = 128
CH = 16
CL = 1024


theta = 10000.0
epsilon = 1e-05
negative = -1e30
far_position = 1073741824
key_block = 1024


def rotate(values, angle_at):
    half_dim = values.shape[-1] // 2
    frequency = theta ** (-(jnp.arange(half_dim, dtype=jnp.float32) * (2.0 / values.shape[-1])))
    angles = angle_at.astype(jnp.float32)[:, None] * frequency[None, :]
    cosine = jnp.cos(angles)[:, None, :]
    sine_term = jnp.sin(angles)[:, None, :]
    first_half = values[..., :half_dim]
    second_half = values[..., half_dim:]
    return jnp.concatenate(
        [
            first_half * cosine - second_half * sine_term,
            second_half * cosine + first_half * sine_term,
        ],
        axis=-1,
    )


def layer_norm(hidden):
    values = hidden.astype(jnp.float32)
    center = values - jnp.mean(values, axis=-1, keepdims=True)
    spread = jnp.mean(center * center, axis=-1, keepdims=True)
    return (center * lax.rsqrt(spread + epsilon)).astype(jnp.bfloat16)


def new_positions(library, span_slot, span_start):
    span_index = library // CL
    span_ids = jnp.arange(CH, dtype=jnp.int32)
    slot_index = jnp.sum(
        jnp.where(span_index[:, None] == span_ids[None, :], span_slot[None, :], 0), axis=1
    )
    start_pos = jnp.sum(
        jnp.where(slot_index[:, None] == span_ids[None, :], span_start[None, :], 0), axis=1
    )
    return start_pos + library % CL


query_tile = 512
log2_e = 1.4426950408889634
key_tile = 4096


def attention_kernel(
    low_limit, high_limit, low_pos, high_pos, q_ref, limit_ref, kv_ref, pos_ref, out_ref,
    peak_ref, total_ref, sum_ref,
):
    query_step = pl.program_id(0)
    key_step = pl.program_id(1)

    @pl.when(key_step == 0)
    def _():
        peak_ref[...] = jnp.full(peak_ref.shape, negative, jnp.float32)
        total_ref[...] = jnp.zeros(total_ref.shape, jnp.float32)
        sum_ref[...] = jnp.zeros(sum_ref.shape, jnp.float32)

    def absorb(masked):
        width = q_ref.shape[1]
        part_keys = kv_ref[:, :width]
        part_values = kv_ref[:, width:]
        scores = lax.dot_general(
            q_ref[...], part_keys, (((1,), (1,)), ((), ())), preferred_element_type=jnp.float32
        ) * (width ** -0.5 * log2_e)
        if masked:
            visible = pos_ref[...] <= limit_ref[...]
            scores = jnp.where(visible, scores, negative)
        old_peak = peak_ref[...]
        new_peak = jnp.maximum(old_peak, jnp.max(scores, axis=1, keepdims=True))
        factor = jnp.exp2(old_peak - new_peak)
        weights = jnp.exp2(scores - new_peak)
        if masked:
            weights = jnp.where(visible, weights, 0.0)
        total_ref[...] = total_ref[...] * factor + jnp.sum(weights, axis=1, keepdims=True)
        sum_ref[...] = sum_ref[...] * factor + jnp.dot(
            weights.astype(jnp.bfloat16), part_values, preferred_element_type=jnp.float32
        )
        peak_ref[...] = new_peak

    all_seen = high_pos[key_step] <= low_limit[query_step]
    none_seen = low_pos[key_step] > high_limit[query_step]

    @pl.when(all_seen)
    def _():
        absorb(False)

    @pl.when(jnp.logical_and(jnp.logical_not(all_seen), jnp.logical_not(none_seen)))
    def _():
        absorb(True)

    @pl.when(key_step == pl.num_programs(1) - 1)
    def _():
        out_ref[...] = (sum_ref[...] / total_ref[...]).astype(out_ref.dtype)


def tile_bounds(query_limit, key_pos):
    rows = query_limit.shape[0]
    count = key_pos.shape[0]
    tiled_limit = query_limit.reshape(rows // min(query_tile, rows), -1)
    tiled_pos = key_pos.reshape(count // min(key_tile, count), -1)
    return (
        jnp.min(tiled_limit, axis=1),
        jnp.max(tiled_limit, axis=1),
        jnp.min(tiled_pos, axis=1),
        jnp.max(tiled_pos, axis=1),
    )


def attend(queries, query_limit, keys_values, key_pos, bounds):
    rows, width = queries.shape
    count = keys_values.shape[0]
    q_tile = min(query_tile, rows)
    k_tile = min(key_tile, count)
    grid_spec = pltpu.PrefetchScalarGridSpec(
        num_scalar_prefetch=4,
        grid=(rows // q_tile, count // k_tile),
        in_specs=[
            pl.BlockSpec((q_tile, width), lambda i, j, *_: (i, 0)),
            pl.BlockSpec((q_tile, 1), lambda i, j, *_: (i, 0)),
            pl.BlockSpec((k_tile, 2 * width), lambda i, j, *_: (j, 0)),
            pl.BlockSpec((1, k_tile), lambda i, j, *_: (0, j)),
        ],
        out_specs=pl.BlockSpec((q_tile, width), lambda i, j, *_: (i, 0)),
        scratch_shapes=[
            pltpu.VMEM((q_tile, 1), jnp.float32),
            pltpu.VMEM((q_tile, 1), jnp.float32),
            pltpu.VMEM((q_tile, width), jnp.float32),
        ],
    )
    return pl.pallas_call(
        attention_kernel,
        grid_spec=grid_spec,
        out_shape=jax.ShapeDtypeStruct((rows, width), jnp.bfloat16),
        compiler_params=pltpu.CompilerParams(
            dimension_semantics=("arbitrary", "arbitrary"), vmem_limit_bytes=48 * 1024 * 1024
        ),
    )(
        *bounds,
        queries,
        query_limit.reshape(rows, 1),
        keys_values,
        key_pos.reshape(1, count),
    )


def online_update(running, queries, query_limit, part_keys, part_values, part_pos):
    run_peak, run_total, run_sum = running
    scores = jnp.einsum(
        "qhd,khd->hqk", queries, part_keys, preferred_element_type=jnp.float32
    ) * HDIM ** (-0.5)
    visible = part_pos[None, None, :] <= query_limit[None, :, None]
    scores = jnp.where(visible, scores, negative)
    new_peak = jnp.maximum(run_peak, jnp.max(scores, axis=-1))
    factor = jnp.exp(run_peak - new_peak)
    weights = jnp.where(visible, jnp.exp(scores - new_peak[..., None]), 0.0)
    run_total = run_total * factor + jnp.sum(weights, axis=-1)
    added = jnp.einsum(
        "hqk,khd->hqd",
        weights.astype(jnp.bfloat16),
        part_values,
        preferred_element_type=jnp.float32,
    )
    run_sum = run_sum * factor[..., None] + added
    return (new_peak, run_total, run_sum)


def local(
    hidden_in,
    cache_keys,
    cache_values,
    w_query,
    w_key,
    w_value,
    w_out,
    span_slot,
    span_start,
    recomp_rows,
):
    head_count = lax.axis_size("head")
    tok_count = lax.axis_size("tok")
    tok_index = lax.axis_index("tok")
    head_index = lax.axis_index("head")
    own_rows = hidden_in.shape[0]
    head_width = w_query.shape[1]
    local_heads = head_width // HDIM
    group_rows = own_rows * head_count
    normed = layer_norm(hidden_in)
    group_slots = lax.dynamic_slice_in_dim(recomp_rows, tok_index * group_rows, group_rows)
    is_live = group_slots >= 0
    query_pos = new_positions(jnp.maximum(group_slots, 0), span_slot, span_start)
    query_limit = jnp.where(is_live, query_pos, far_position)
    count_keys = cache_keys.shape[0] * head_count * tok_count
    all_pos = new_positions(jnp.arange(count_keys, dtype=jnp.int32), span_slot, span_start)
    bounds = tile_bounds(query_limit, all_pos)
    block_len = cache_keys.shape[0] * head_count
    target = jnp.where(is_live, group_slots - tok_index * block_len, block_len)
    picks = jnp.arange(block_len, dtype=jnp.int32)[:, None] == target[None, :]
    pick_weights = picks.astype(jnp.bfloat16)
    replaced = jnp.any(picks, axis=1)[:, None]
    after_bounds = -(
        jnp.abs(sum(bound[0] for bound in bounds).astype(jnp.bfloat16) + pick_weights[-1, -1]) * 0
    )
    w_joined = jnp.concatenate([w_query, w_key, w_value], axis=1) + after_bounds
    projected = jnp.dot(
        lax.all_gather(normed, "head", axis=0, tiled=True),
        w_joined,
        preferred_element_type=jnp.float32,
    )
    queries = rotate(
        projected[:, :head_width].reshape(group_rows, local_heads, HDIM), query_pos
    ).astype(jnp.bfloat16)
    fresh_keys = rotate(
        projected[:, head_width : 2 * head_width].reshape(group_rows, local_heads, HDIM), query_pos
    ).astype(jnp.bfloat16)
    fresh_values = (
        projected[:, 2 * head_width :].astype(jnp.bfloat16).reshape(group_rows, local_heads, HDIM)
    )
    moved_keys, moved_values = (
        lax.all_to_all(cache_keys, "head", split_axis=1, concat_axis=0, tiled=True),
        lax.all_to_all(cache_values, "head", split_axis=1, concat_axis=0, tiled=True),
    )
    block_len = moved_keys.shape[0]
    library = tok_index * block_len + jnp.arange(block_len, dtype=jnp.int32)
    key_pos = new_positions(library, span_slot, span_start)
    shifted = rotate(
        moved_keys.astype(jnp.float32).reshape(block_len, local_heads, HDIM), key_pos - library % CL
    ).astype(jnp.bfloat16)
    fresh_both = jnp.concatenate(
        [fresh_keys.reshape(group_rows, head_width), fresh_values.reshape(group_rows, head_width)], axis=1
    )
    picked = jnp.dot(
        pick_weights, fresh_both, preferred_element_type=jnp.float32
    ).astype(jnp.bfloat16)
    merged_both = jnp.where(
        replaced,
        picked,
        jnp.concatenate([shifted.reshape(block_len, head_width), moved_values], axis=1),
    )
    merged_keys = merged_both[:, :head_width]
    merged_values = merged_both[:, head_width:]
    all_both = lax.all_gather(merged_both, "tok", axis=0, tiled=True)

    def head_columns(both, head):
        if local_heads == 1:
            return both
        return jnp.concatenate(
            [
                both[:, head * HDIM : (head + 1) * HDIM],
                both[:, head_width + head * HDIM : head_width + (head + 1) * HDIM],
            ],
            axis=1,
        )

    attended_heads = [
        attend(queries[:, head], query_limit, head_columns(all_both, head), all_pos, bounds)
        for head in range(local_heads)
    ]
    attended = jnp.concatenate(attended_heads, axis=1)
    out_width = w_out.shape[1]
    column_half = tok_index % 2
    after_gather = -(jnp.abs(all_both[0, 0]) * 0)
    own_half = lax.all_gather(
        lax.dynamic_slice_in_dim(w_out, column_half * (out_width // 2), out_width // 2, 1)
        + after_gather,
        "head",
        axis=0,
        tiled=True,
    )
    partner_pairs = [(i, i ^ 1) for i in range(tok_count)]
    slot_rows = lax.all_to_all(attended, "head", split_axis=0, concat_axis=1, tiled=True)
    partner_rows = lax.ppermute(slot_rows, "tok", partner_pairs)
    both_parts = jnp.dot(
        jnp.concatenate([slot_rows, partner_rows], axis=0), own_half, preferred_element_type=jnp.float32
    ).astype(jnp.bfloat16)
    mine = both_parts[:own_rows]
    other = lax.ppermute(both_parts[own_rows:], "tok", partner_pairs)
    update = jnp.where(
        column_half == 0,
        jnp.concatenate([mine, other], axis=1),
        jnp.concatenate([other, mine], axis=1),
    )
    own_slots = lax.dynamic_slice_in_dim(
        recomp_rows, (tok_index * head_count + head_index) * own_rows, own_rows
    )
    update = jnp.where((own_slots >= 0)[:, None], update, 0.0).astype(jnp.bfloat16)
    return (update, merged_keys, merged_values)


def solution(mesh):
    in_specs = (
        P(("tok", "head"), None),
        P(("tok", "head"), None),
        P(("tok", "head"), None),
        P(None, "head"),
        P(None, "head"),
        P(None, "head"),
        P("head", None),
        P(),
        P(),
        P(),
    )
    out_specs = (P(("tok", "head"), None), P("tok", "head"), P("tok", "head"))
    return jax.shard_map(local, mesh=mesh, in_specs=in_specs, out_specs=out_specs, check_vma=False)
```

```python
import functools

import jax
import jax.numpy as jnp
from jax import lax
from jax.sharding import PartitionSpec as P
from jax.experimental import pallas as pl
from jax.experimental.pallas import tpu as pltpu

HDIM = 128
CH = 16
CL = 1024


theta = 10000.0
epsilon = 1e-05
negative = -1e30
far_position = 1073741824
key_block = 1024


def rotate(values, angle_at):
    half_dim = values.shape[-1] // 2
    frequency = theta ** (-(jnp.arange(half_dim, dtype=jnp.float32) * (2.0 / values.shape[-1])))
    angles = angle_at.astype(jnp.float32)[:, None] * frequency[None, :]
    cosine = jnp.cos(angles)[:, None, :]
    sine_term = jnp.sin(angles)[:, None, :]
    first_half = values[..., :half_dim]
    second_half = values[..., half_dim:]
    return jnp.concatenate(
        [
            first_half * cosine - second_half * sine_term,
            second_half * cosine + first_half * sine_term,
        ],
        axis=-1,
    )


def layer_norm(hidden):
    values = hidden.astype(jnp.float32)
    center = values - jnp.mean(values, axis=-1, keepdims=True)
    spread = jnp.mean(center * center, axis=-1, keepdims=True)
    return (center * lax.rsqrt(spread + epsilon)).astype(jnp.bfloat16)


def new_positions(library, span_slot, span_start):
    span_index = library // CL
    span_ids = jnp.arange(CH, dtype=jnp.int32)
    slot_index = jnp.sum(
        jnp.where(span_index[:, None] == span_ids[None, :], span_slot[None, :], 0), axis=1
    )
    start_pos = jnp.sum(
        jnp.where(slot_index[:, None] == span_ids[None, :], span_start[None, :], 0), axis=1
    )
    return start_pos + library % CL


query_tile = 512
log2_e = 1.4426950408889634
key_tile = 4096


def attention_kernel(
    low_limit, high_limit, low_pos, high_pos, q_ref, limit_ref, kv_ref, pos_ref, out_ref,
    peak_ref, total_ref, sum_ref,
):
    query_step = pl.program_id(0)
    key_step = pl.program_id(1)

    @pl.when(key_step == 0)
    def _():
        peak_ref[...] = jnp.full(peak_ref.shape, negative, jnp.float32)
        total_ref[...] = jnp.zeros(total_ref.shape, jnp.float32)
        sum_ref[...] = jnp.zeros(sum_ref.shape, jnp.float32)

    def absorb(masked):
        width = q_ref.shape[1]
        part_keys = kv_ref[:, :width]
        part_values = kv_ref[:, width:]
        scores = lax.dot_general(
            q_ref[...], part_keys, (((1,), (1,)), ((), ())), preferred_element_type=jnp.float32
        ) * (width ** -0.5 * log2_e)
        if masked:
            visible = pos_ref[...] <= limit_ref[...]
            scores = jnp.where(visible, scores, negative)
        old_peak = peak_ref[...]
        new_peak = jnp.maximum(old_peak, jnp.max(scores, axis=1, keepdims=True))
        factor = jnp.exp2(old_peak - new_peak)
        weights = jnp.exp2(scores - new_peak)
        if masked:
            weights = jnp.where(visible, weights, 0.0)
        total_ref[...] = total_ref[...] * factor + jnp.sum(weights, axis=1, keepdims=True)
        sum_ref[...] = sum_ref[...] * factor + jnp.dot(
            weights.astype(jnp.bfloat16), part_values, preferred_element_type=jnp.float32
        )
        peak_ref[...] = new_peak

    all_seen = high_pos[key_step] <= low_limit[query_step]
    none_seen = low_pos[key_step] > high_limit[query_step]

    @pl.when(all_seen)
    def _():
        absorb(False)

    @pl.when(jnp.logical_and(jnp.logical_not(all_seen), jnp.logical_not(none_seen)))
    def _():
        absorb(True)

    @pl.when(key_step == pl.num_programs(1) - 1)
    def _():
        out_ref[...] = (sum_ref[...] / total_ref[...]).astype(out_ref.dtype)


def tile_bounds(query_limit, key_pos):
    rows = query_limit.shape[0]
    count = key_pos.shape[0]
    tiled_limit = query_limit.reshape(rows // min(query_tile, rows), -1)
    tiled_pos = key_pos.reshape(count // min(key_tile, count), -1)
    return (
        jnp.min(tiled_limit, axis=1),
        jnp.max(tiled_limit, axis=1),
        jnp.min(tiled_pos, axis=1),
        jnp.max(tiled_pos, axis=1),
    )


def attend(queries, query_limit, keys_values, key_pos, bounds):
    rows, width = queries.shape
    count = keys_values.shape[0]
    q_tile = min(query_tile, rows)
    k_tile = min(key_tile, count)
    grid_spec = pltpu.PrefetchScalarGridSpec(
        num_scalar_prefetch=4,
        grid=(rows // q_tile, count // k_tile),
        in_specs=[
            pl.BlockSpec((q_tile, width), lambda i, j, *_: (i, 0)),
            pl.BlockSpec((q_tile, 1), lambda i, j, *_: (i, 0)),
            pl.BlockSpec((k_tile, 2 * width), lambda i, j, *_: (j, 0)),
            pl.BlockSpec((1, k_tile), lambda i, j, *_: (0, j)),
        ],
        out_specs=pl.BlockSpec((q_tile, width), lambda i, j, *_: (i, 0)),
        scratch_shapes=[
            pltpu.VMEM((q_tile, 1), jnp.float32),
            pltpu.VMEM((q_tile, 1), jnp.float32),
            pltpu.VMEM((q_tile, width), jnp.float32),
        ],
    )
    return pl.pallas_call(
        attention_kernel,
        grid_spec=grid_spec,
        out_shape=jax.ShapeDtypeStruct((rows, width), jnp.bfloat16),
        compiler_params=pltpu.CompilerParams(
            dimension_semantics=("arbitrary", "arbitrary"), vmem_limit_bytes=48 * 1024 * 1024
        ),
    )(
        *bounds,
        queries,
        query_limit.reshape(rows, 1),
        keys_values,
        key_pos.reshape(1, count),
    )


def online_update(running, queries, query_limit, part_keys, part_values, part_pos):
    run_peak, run_total, run_sum = running
    scores = jnp.einsum(
        "qhd,khd->hqk", queries, part_keys, preferred_element_type=jnp.float32
    ) * HDIM ** (-0.5)
    visible = part_pos[None, None, :] <= query_limit[None, :, None]
    scores = jnp.where(visible, scores, negative)
    new_peak = jnp.maximum(run_peak, jnp.max(scores, axis=-1))
    factor = jnp.exp(run_peak - new_peak)
    weights = jnp.where(visible, jnp.exp(scores - new_peak[..., None]), 0.0)
    run_total = run_total * factor + jnp.sum(weights, axis=-1)
    added = jnp.einsum(
        "hqk,khd->hqd",
        weights.astype(jnp.bfloat16),
        part_values,
        preferred_element_type=jnp.float32,
    )
    run_sum = run_sum * factor[..., None] + added
    return (new_peak, run_total, run_sum)


def local(
    hidden_in,
    cache_keys,
    cache_values,
    w_query,
    w_key,
    w_value,
    w_out,
    span_slot,
    span_start,
    recomp_rows,
):
    head_count = lax.axis_size("head")
    tok_count = lax.axis_size("tok")
    tok_index = lax.axis_index("tok")
    head_index = lax.axis_index("head")
    own_rows = hidden_in.shape[0]
    head_width = w_query.shape[1]
    local_heads = head_width // HDIM
    group_rows = own_rows * head_count
    normed = layer_norm(hidden_in)
    group_slots = lax.dynamic_slice_in_dim(recomp_rows, tok_index * group_rows, group_rows)
    is_live = group_slots >= 0
    query_pos = new_positions(jnp.maximum(group_slots, 0), span_slot, span_start)
    query_limit = jnp.where(is_live, query_pos, far_position)
    count_keys = cache_keys.shape[0] * head_count * tok_count
    all_pos = new_positions(jnp.arange(count_keys, dtype=jnp.int32), span_slot, span_start)
    bounds = tile_bounds(query_limit, all_pos)
    block_len = cache_keys.shape[0] * head_count
    target = jnp.where(is_live, group_slots - tok_index * block_len, block_len)
    picks = jnp.arange(block_len, dtype=jnp.int32)[:, None] == target[None, :]
    pick_weights = picks.astype(jnp.bfloat16)
    replaced = jnp.any(picks, axis=1)[:, None]
    after_bounds = -(
        jnp.abs(sum(bound[0] for bound in bounds).astype(jnp.bfloat16) + pick_weights[-1, -1]) * 0
    )
    w_joined = jnp.concatenate([w_query, w_key, w_value], axis=1) + after_bounds
    projected = jnp.dot(
        lax.all_gather(normed, "head", axis=0, tiled=True),
        w_joined,
        preferred_element_type=jnp.float32,
    )
    queries = rotate(
        projected[:, :head_width].reshape(group_rows, local_heads, HDIM), query_pos
    ).astype(jnp.bfloat16)
    fresh_keys = rotate(
        projected[:, head_width : 2 * head_width].reshape(group_rows, local_heads, HDIM), query_pos
    ).astype(jnp.bfloat16)
    fresh_values = (
        projected[:, 2 * head_width :].astype(jnp.bfloat16).reshape(group_rows, local_heads, HDIM)
    )
    moved_keys, moved_values = (
        lax.all_to_all(cache_keys, "head", split_axis=1, concat_axis=0, tiled=True),
        lax.all_to_all(cache_values, "head", split_axis=1, concat_axis=0, tiled=True),
    )
    block_len = moved_keys.shape[0]
    library = tok_index * block_len + jnp.arange(block_len, dtype=jnp.int32)
    key_pos = new_positions(library, span_slot, span_start)
    shifted = rotate(
        moved_keys.astype(jnp.float32).reshape(block_len, local_heads, HDIM), key_pos - library % CL
    ).astype(jnp.bfloat16)
    fresh_both = jnp.concatenate(
        [fresh_keys.reshape(group_rows, head_width), fresh_values.reshape(group_rows, head_width)], axis=1
    )
    picked = jnp.dot(
        pick_weights, fresh_both, preferred_element_type=jnp.float32
    ).astype(jnp.bfloat16)
    merged_both = jnp.where(
        replaced,
        picked,
        jnp.concatenate([shifted.reshape(block_len, head_width), moved_values], axis=1),
    )
    merged_keys = merged_both[:, :head_width]
    merged_values = merged_both[:, head_width:]
    all_both = lax.all_gather(merged_both, "tok", axis=0, tiled=True)

    def head_columns(both, head):
        if local_heads == 1:
            return both
        return jnp.concatenate(
            [
                both[:, head * HDIM : (head + 1) * HDIM],
                both[:, head_width + head * HDIM : head_width + (head + 1) * HDIM],
            ],
            axis=1,
        )

    attended_heads = [
        attend(queries[:, head], query_limit, head_columns(all_both, head), all_pos, bounds)
        for head in range(local_heads)
    ]
    attended = jnp.concatenate(attended_heads, axis=1)
    out_width = w_out.shape[1]
    column_half = tok_index % 2
    after_gather = -(jnp.abs(merged_both[-1, -1]) * 0)
    own_half = lax.all_gather(
        lax.dynamic_slice_in_dim(w_out, column_half * (out_width // 2), out_width // 2, 1)
        + after_gather,
        "head",
        axis=0,
        tiled=True,
    )
    partner_pairs = [(i, i ^ 1) for i in range(tok_count)]
    slot_rows = lax.all_to_all(attended, "head", split_axis=0, concat_axis=1, tiled=True)
    partner_rows = lax.ppermute(slot_rows, "tok", partner_pairs)
    both_parts = jnp.dot(
        jnp.concatenate([slot_rows, partner_rows], axis=0), own_half, preferred_element_type=jnp.float32
    ).astype(jnp.bfloat16)
    mine = both_parts[:own_rows]
    other = lax.ppermute(both_parts[own_rows:], "tok", partner_pairs)
    update = jnp.where(
        column_half == 0,
        jnp.concatenate([mine, other], axis=1),
        jnp.concatenate([other, mine], axis=1),
    )
    own_slots = lax.dynamic_slice_in_dim(
        recomp_rows, (tok_index * head_count + head_index) * own_rows, own_rows
    )
    update = jnp.where((own_slots >= 0)[:, None], update, 0.0).astype(jnp.bfloat16)
    return (update, merged_keys, merged_values)


def solution(mesh):
    in_specs = (
        P(("tok", "head"), None),
        P(("tok", "head"), None),
        P(("tok", "head"), None),
        P(None, "head"),
        P(None, "head"),
        P(None, "head"),
        P("head", None),
        P(),
        P(),
        P(),
    )
    out_specs = (P(("tok", "head"), None), P("tok", "head"), P("tok", "head"))
    return jax.shard_map(local, mesh=mesh, in_specs=in_specs, out_specs=out_specs, check_vma=False)
```

```python
import functools

import jax
import jax.numpy as jnp
from jax import lax
from jax.sharding import PartitionSpec as P
from jax.experimental import pallas as pl
from jax.experimental.pallas import tpu as pltpu

HDIM = 128
CH = 16
CL = 1024


theta = 10000.0
epsilon = 1e-05
negative = -1e30
far_position = 1073741824
key_block = 1024


def rotate(values, angle_at):
    half_dim = values.shape[-1] // 2
    frequency = theta ** (-(jnp.arange(half_dim, dtype=jnp.float32) * (2.0 / values.shape[-1])))
    angles = angle_at.astype(jnp.float32)[:, None] * frequency[None, :]
    cosine = jnp.cos(angles)[:, None, :]
    sine_term = jnp.sin(angles)[:, None, :]
    first_half = values[..., :half_dim]
    second_half = values[..., half_dim:]
    return jnp.concatenate(
        [
            first_half * cosine - second_half * sine_term,
            second_half * cosine + first_half * sine_term,
        ],
        axis=-1,
    )


def layer_norm(hidden):
    values = hidden.astype(jnp.float32)
    center = values - jnp.mean(values, axis=-1, keepdims=True)
    spread = jnp.mean(center * center, axis=-1, keepdims=True)
    return (center * lax.rsqrt(spread + epsilon)).astype(jnp.bfloat16)


def new_positions(library, span_slot, span_start):
    span_index = library // CL
    span_ids = jnp.arange(CH, dtype=jnp.int32)
    slot_index = jnp.sum(
        jnp.where(span_index[:, None] == span_ids[None, :], span_slot[None, :], 0), axis=1
    )
    start_pos = jnp.sum(
        jnp.where(slot_index[:, None] == span_ids[None, :], span_start[None, :], 0), axis=1
    )
    return start_pos + library % CL


query_tile = 512
log2_e = 1.4426950408889634
key_tile = 4096


def attention_kernel(
    low_limit, high_limit, low_pos, high_pos, q_ref, limit_ref, kv_ref, pos_ref, out_ref,
    peak_ref, total_ref, sum_ref,
):
    query_step = pl.program_id(0)
    key_step = pl.program_id(1)

    @pl.when(key_step == 0)
    def _():
        peak_ref[...] = jnp.full(peak_ref.shape, negative, jnp.float32)
        total_ref[...] = jnp.zeros(total_ref.shape, jnp.float32)
        sum_ref[...] = jnp.zeros(sum_ref.shape, jnp.float32)

    def absorb(masked):
        width = q_ref.shape[1]
        part_keys = kv_ref[:, :width]
        part_values = kv_ref[:, width:]
        scores = lax.dot_general(
            q_ref[...], part_keys, (((1,), (1,)), ((), ())), preferred_element_type=jnp.float32
        ) * (width ** -0.5 * log2_e)
        if masked:
            visible = pos_ref[...] <= limit_ref[...]
            scores = jnp.where(visible, scores, negative)
        old_peak = peak_ref[...]
        new_peak = jnp.maximum(old_peak, jnp.max(scores, axis=1, keepdims=True))
        factor = jnp.exp2(old_peak - new_peak)
        weights = jnp.exp2(scores - new_peak)
        if masked:
            weights = jnp.where(visible, weights, 0.0)
        total_ref[...] = total_ref[...] * factor + jnp.sum(weights, axis=1, keepdims=True)
        sum_ref[...] = sum_ref[...] * factor + jnp.dot(
            weights.astype(jnp.bfloat16), part_values, preferred_element_type=jnp.float32
        )
        peak_ref[...] = new_peak

    all_seen = high_pos[key_step] <= low_limit[query_step]
    none_seen = low_pos[key_step] > high_limit[query_step]

    @pl.when(all_seen)
    def _():
        absorb(False)

    @pl.when(jnp.logical_and(jnp.logical_not(all_seen), jnp.logical_not(none_seen)))
    def _():
        absorb(True)

    @pl.when(key_step == pl.num_programs(1) - 1)
    def _():
        out_ref[...] = (sum_ref[...] / total_ref[...]).astype(out_ref.dtype)


def tile_bounds(query_limit, key_pos):
    rows = query_limit.shape[0]
    count = key_pos.shape[0]
    tiled_limit = query_limit.reshape(rows // min(query_tile, rows), -1)
    tiled_pos = key_pos.reshape(count // min(key_tile, count), -1)
    return (
        jnp.min(tiled_limit, axis=1),
        jnp.max(tiled_limit, axis=1),
        jnp.min(tiled_pos, axis=1),
        jnp.max(tiled_pos, axis=1),
    )


def attend(queries, query_limit, keys_values, key_pos, bounds):
    rows, width = queries.shape
    count = keys_values.shape[0]
    q_tile = min(query_tile, rows)
    k_tile = min(key_tile, count)
    grid_spec = pltpu.PrefetchScalarGridSpec(
        num_scalar_prefetch=4,
        grid=(rows // q_tile, count // k_tile),
        in_specs=[
            pl.BlockSpec((q_tile, width), lambda i, j, *_: (i, 0)),
            pl.BlockSpec((q_tile, 1), lambda i, j, *_: (i, 0)),
            pl.BlockSpec((k_tile, 2 * width), lambda i, j, *_: (j, 0)),
            pl.BlockSpec((1, k_tile), lambda i, j, *_: (0, j)),
        ],
        out_specs=pl.BlockSpec((q_tile, width), lambda i, j, *_: (i, 0)),
        scratch_shapes=[
            pltpu.VMEM((q_tile, 1), jnp.float32),
            pltpu.VMEM((q_tile, 1), jnp.float32),
            pltpu.VMEM((q_tile, width), jnp.float32),
        ],
    )
    return pl.pallas_call(
        attention_kernel,
        grid_spec=grid_spec,
        out_shape=jax.ShapeDtypeStruct((rows, width), jnp.bfloat16),
        compiler_params=pltpu.CompilerParams(
            dimension_semantics=("arbitrary", "arbitrary"), vmem_limit_bytes=48 * 1024 * 1024
        ),
    )(
        *bounds,
        queries,
        query_limit.reshape(rows, 1),
        keys_values,
        key_pos.reshape(1, count),
    )


def online_update(running, queries, query_limit, part_keys, part_values, part_pos):
    run_peak, run_total, run_sum = running
    scores = jnp.einsum(
        "qhd,khd->hqk", queries, part_keys, preferred_element_type=jnp.float32
    ) * HDIM ** (-0.5)
    visible = part_pos[None, None, :] <= query_limit[None, :, None]
    scores = jnp.where(visible, scores, negative)
    new_peak = jnp.maximum(run_peak, jnp.max(scores, axis=-1))
    factor = jnp.exp(run_peak - new_peak)
    weights = jnp.where(visible, jnp.exp(scores - new_peak[..., None]), 0.0)
    run_total = run_total * factor + jnp.sum(weights, axis=-1)
    added = jnp.einsum(
        "hqk,khd->hqd",
        weights.astype(jnp.bfloat16),
        part_values,
        preferred_element_type=jnp.float32,
    )
    run_sum = run_sum * factor[..., None] + added
    return (new_peak, run_total, run_sum)


def local(
    hidden_in,
    cache_keys,
    cache_values,
    w_query,
    w_key,
    w_value,
    w_out,
    span_slot,
    span_start,
    recomp_rows,
):
    head_count = lax.axis_size("head")
    tok_count = lax.axis_size("tok")
    tok_index = lax.axis_index("tok")
    head_index = lax.axis_index("head")
    own_rows = hidden_in.shape[0]
    head_width = w_query.shape[1]
    local_heads = head_width // HDIM
    group_rows = own_rows * head_count
    normed = layer_norm(hidden_in)
    group_slots = lax.dynamic_slice_in_dim(recomp_rows, tok_index * group_rows, group_rows)
    is_live = group_slots >= 0
    query_pos = new_positions(jnp.maximum(group_slots, 0), span_slot, span_start)
    query_limit = jnp.where(is_live, query_pos, far_position)
    count_keys = cache_keys.shape[0] * head_count * tok_count
    all_pos = new_positions(jnp.arange(count_keys, dtype=jnp.int32), span_slot, span_start)
    bounds = tile_bounds(query_limit, all_pos)
    block_len = cache_keys.shape[0] * head_count
    target = jnp.where(is_live, group_slots - tok_index * block_len, block_len)
    picks = jnp.arange(block_len, dtype=jnp.int32)[:, None] == target[None, :]
    pick_weights = picks.astype(jnp.bfloat16)
    replaced = jnp.any(picks, axis=1)[:, None]
    after_bounds = -(
        jnp.abs(sum(bound[0] for bound in bounds).astype(jnp.bfloat16) + pick_weights[-1, -1]) * 0
    )
    gathered = lax.all_gather(normed, "head", axis=0, tiled=True)
    projected = jnp.dot(
        gathered,
        jnp.concatenate([w_key, w_value], axis=1) + after_bounds,
        preferred_element_type=jnp.float32,
    )
    query_projected = jnp.dot(gathered, w_query, preferred_element_type=jnp.float32)
    queries = rotate(
        query_projected.reshape(group_rows, local_heads, HDIM), query_pos
    ).astype(jnp.bfloat16)
    fresh_keys = rotate(
        projected[:, :head_width].reshape(group_rows, local_heads, HDIM), query_pos
    ).astype(jnp.bfloat16)
    fresh_values = (
        projected[:, head_width:].astype(jnp.bfloat16).reshape(group_rows, local_heads, HDIM)
    )
    moved_keys, moved_values = (
        lax.all_to_all(cache_keys, "head", split_axis=1, concat_axis=0, tiled=True),
        lax.all_to_all(cache_values, "head", split_axis=1, concat_axis=0, tiled=True),
    )
    block_len = moved_keys.shape[0]
    library = tok_index * block_len + jnp.arange(block_len, dtype=jnp.int32)
    key_pos = new_positions(library, span_slot, span_start)
    shifted = rotate(
        moved_keys.astype(jnp.float32).reshape(block_len, local_heads, HDIM), key_pos - library % CL
    ).astype(jnp.bfloat16)
    fresh_both = jnp.concatenate(
        [fresh_keys.reshape(group_rows, head_width), fresh_values.reshape(group_rows, head_width)], axis=1
    )
    picked = jnp.dot(
        pick_weights, fresh_both, preferred_element_type=jnp.float32
    ).astype(jnp.bfloat16)
    merged_both = jnp.where(
        replaced,
        picked,
        jnp.concatenate([shifted.reshape(block_len, head_width), moved_values], axis=1),
    )
    merged_keys = merged_both[:, :head_width]
    merged_values = merged_both[:, head_width:]
    all_both = lax.all_gather(merged_both, "tok", axis=0, tiled=True)

    def head_columns(both, head):
        if local_heads == 1:
            return both
        return jnp.concatenate(
            [
                both[:, head * HDIM : (head + 1) * HDIM],
                both[:, head_width + head * HDIM : head_width + (head + 1) * HDIM],
            ],
            axis=1,
        )

    attended_heads = [
        attend(queries[:, head], query_limit, head_columns(all_both, head), all_pos, bounds)
        for head in range(local_heads)
    ]
    attended = jnp.concatenate(attended_heads, axis=1)
    out_width = w_out.shape[1]
    column_half = tok_index % 2
    after_gather = -(jnp.abs(merged_both[-1, -1]) * 0)
    own_half = lax.all_gather(
        lax.dynamic_slice_in_dim(w_out, column_half * (out_width // 2), out_width // 2, 1)
        + after_gather,
        "head",
        axis=0,
        tiled=True,
    )
    partner_pairs = [(i, i ^ 1) for i in range(tok_count)]
    slot_rows = lax.all_to_all(attended, "head", split_axis=0, concat_axis=1, tiled=True)
    partner_rows = lax.ppermute(slot_rows, "tok", partner_pairs)
    both_parts = jnp.dot(
        jnp.concatenate([slot_rows, partner_rows], axis=0), own_half, preferred_element_type=jnp.float32
    ).astype(jnp.bfloat16)
    mine = both_parts[:own_rows]
    other = lax.ppermute(both_parts[own_rows:], "tok", partner_pairs)
    update = jnp.where(
        column_half == 0,
        jnp.concatenate([mine, other], axis=1),
        jnp.concatenate([other, mine], axis=1),
    )
    own_slots = lax.dynamic_slice_in_dim(
        recomp_rows, (tok_index * head_count + head_index) * own_rows, own_rows
    )
    update = jnp.where((own_slots >= 0)[:, None], update, 0.0).astype(jnp.bfloat16)
    return (update, merged_keys, merged_values)


def solution(mesh):
    in_specs = (
        P(("tok", "head"), None),
        P(("tok", "head"), None),
        P(("tok", "head"), None),
        P(None, "head"),
        P(None, "head"),
        P(None, "head"),
        P("head", None),
        P(),
        P(),
        P(),
    )
    out_specs = (P(("tok", "head"), None), P("tok", "head"), P("tok", "head"))
    return jax.shard_map(local, mesh=mesh, in_specs=in_specs, out_specs=out_specs, check_vma=False)
```
